256 devices in a mesh: gx: 8 (over x, core), gy: 32 (over y, z).
Axes of the slice: x: 4, y: 4, z: 8, core: 2. Of those that a mesh axis runs over, the one named last changes fastest.
Arguments:
- hidden_in: bfloat16 [8192, 4096], P('gx', 'gy')
- norm_gain: bfloat16 [4096], P('gy'), may hold values from 0.099609375 to 1.8984375
- query_proj: bfloat16 [4096, 4096], P('gx', 'gy')
- kv_proj: bfloat16 [1024, 4096], P(None, 'gy')
- prompt_lengths: int32 [8], replicated, may hold values from 1 to 4096, 8192 in all
- cache_slot: int32 [512], replicated, may hold values from 0 to 511, as said below
Outputs:
- attention: bfloat16 [8192, 4096], P('gy', 'gx')
- kv_cache: bfloat16 [512, 16, 1024], P('gy', None, 'gx')
The draws below stay inside these ranges and needn't reach their ends.
Inputs may be any that keep to these rules, and one draw needn't show every extreme that they name: `prompt_lengths`: the 8 prompts sum to 8192 tokens; the longest has exactly 4096. `cache_slot`: A permutation of the 512 slots; slot s is held by index s // 16 of gy. The 16 pages of one token block go to any one index at most 1 times, and every index receives exactly 16 pages.
All inputs are finite; a program needn't handle non-finite values.
Results may differ from the reference program's by a relative error of at most 0.0066.
The reference program's roundings to bfloat16 on the way (of `normed`, `queries` and `rounded`) count: a program that leaves them out, or rounds other values in their place, can miss the bound.
Values may be sent and summed in bfloat16 or wider, within the bound.
No kernel may reach another device: no remote copies, remote signals or barrier semaphores. Data moves between devices by JAX's collectives and lax.ppermute only.
A program may use at most 128 MiB of HBM per device.

```python
import math
import jax
import jax.numpy as jnp
import numpy as np
from jax import lax

D = 4096
H = 32
KVH = 4
HD = 128
TOK_BLK = 256
PAGES_DEV = 16
NSEG = 8
TOKENS = 8192
MOST = 4096
PAGE = 16
PAGES = 512


def draw_hidden_in(key, part):
    noise_key = jax.random.fold_in(key, 1)
    row_key = jax.random.fold_in(key, 2)
    column_key = jax.random.fold_in(key, 3)
    column_scale = 3.0 ** (jnp.arange(D, dtype=jnp.float32) / (D - 1)) * jnp.exp(jax.random.uniform(column_key, (D,)) * math.log(10.0))
    noise_draw = jax.random.normal(noise_key, (TOKENS, D))
    row_scale = jnp.exp(jax.random.uniform(row_key, (TOKENS,)) * math.log(10.0))
    return (0.1 * noise_draw * row_scale[:, None] * column_scale[None, :]).astype(jnp.bfloat16)


def kv_matrix(key):
    kv_key = jax.random.fold_in(key, 11)
    noise_draw = jax.random.normal(kv_key, (2 * KVH * HD, D))
    return noise_draw * D ** (-0.5)


def draw_kv_proj(key, part):
    return kv_matrix(key).astype(jnp.bfloat16)


def draw_query_proj(key, part):
    query_key = jax.random.fold_in(key, 12)
    noise_draw = jax.random.normal(query_key, (H * HD, D)) * D ** (-0.5)
    return noise_draw.astype(jnp.bfloat16)


def draw_cache_slot(key, part):
    per_dev = PAGES_DEV
    owner_count = PAGES // PAGES_DEV
    first_perm = jax.random.permutation(jax.random.fold_in(key, 21), owner_count)
    second_perm = jax.random.permutation(jax.random.fold_in(key, 22), owner_count)
    offsets = jax.random.permutation(jax.random.fold_in(key, 23), max(owner_count, per_dev))[:per_dev] % owner_count
    owners = second_perm[(first_perm[:, None] + offsets[None, :]) % owner_count]
    scores = jax.random.randint(jax.random.fold_in(key, 24), (owner_count, per_dev), 0, 1 << 20) * per_dev + jnp.arange(per_dev, dtype=jnp.int32)[None, :]
    order_rank = jnp.argsort(jnp.argsort(scores, axis=1), axis=1)
    local_slot = order_rank[owners, jnp.arange(per_dev, dtype=jnp.int32)[None, :]]
    return (owners * per_dev + local_slot).reshape(-1).astype(jnp.int32)


def length_profile(amount, total, limit, lean):
    weights = [(1 << 20) // math.isqrt(grade ** lean) + 1 for grade in range(2, amount + 1)]
    rest, counts = total - limit - (amount - 1), [1] * (amount - 1)
    while rest > 0:
        candidates = [i for i in range(amount - 1) if counts[i] < limit]
        mass, left = sum([weights[i] for i in candidates]), rest
        for i in candidates:
            extra = min(limit - counts[i], max(1, left * weights[i] // mass), rest)
            counts[i] = counts[i] + extra
            rest = rest - extra
    return np.array([limit] + counts)


def ragged(own_key, count, total, reach, slope):
    if count == 2:
        one = jax.random.randint(own_key, (), max(1, total - reach), min(reach, total - 1) + 1)
        return jnp.stack([one, total - one])
    tallies = jnp.asarray(length_profile(count, total, reach, slope), jnp.int32)
    couples = (count - 1) // 2
    source_of, receiver = tallies[1:1 + 2 * couples:2], tallies[2:2 + 2 * couples:2]
    room = jnp.minimum(source_of - 1, reach - receiver)
    passed = jax.random.randint(jax.random.fold_in(own_key, 1), (couples,), 0, 1 << 20) % (room + 1)
    tallies = tallies.at[1:1 + 2 * couples:2].set(source_of - passed).at[2:2 + 2 * couples:2].set(receiver + passed)
    return tallies[jax.random.permutation(jax.random.fold_in(own_key, 2), count)]


def setup_inputs(seed: int = 0) -> dict:
    arg_keys = jax.random.split(jax.random.key(seed), 7)
    return {
        "hidden_in": draw_hidden_in(jax.random.fold_in(arg_keys[6], 71), 0),
        "norm_gain": jnp.clip(1.0 + 0.18 * jax.random.normal(arg_keys[1], (D,), jnp.float32), 0.099609375, 1.8984375).astype(jnp.bfloat16),
        "query_proj": draw_query_proj(jax.random.fold_in(arg_keys[6], 71), 0),
        "kv_proj": draw_kv_proj(jax.random.fold_in(arg_keys[6], 71), 0),
        "prompt_lengths": ragged(arg_keys[4], NSEG, TOKENS, MOST, 2).astype(jnp.int32),
        "cache_slot": draw_cache_slot(jax.random.fold_in(arg_keys[6], 71), 0),
    }


epsilon = 1e-06
rope_base = 5000000.0
masked_out = -1e+30

def token_places(prompt_lengths, token_index):
    prompt_ends = jnp.cumsum(prompt_lengths).astype(jnp.int32)
    prompt_starts = prompt_ends - prompt_lengths
    segment = lax.optimization_barrier(jnp.sum((token_index[:, None] >= prompt_ends[None, :]).astype(jnp.int32), axis=1))
    chosen = segment[:, None] == jnp.arange(prompt_lengths.shape[0], dtype=jnp.int32)[None, :]
    opening = lax.optimization_barrier(jnp.sum(jnp.where(chosen, prompt_starts[None, :], 0), axis=1)).astype(jnp.int32)
    return (segment, token_index - opening)

def rotate(vectors, places):
    half_size = vectors.shape[-1] // 2
    frequency = rope_base ** (-(jnp.arange(half_size, dtype=jnp.float32) * 2.0) / vectors.shape[-1])
    angles = places.astype(jnp.float32)[:, None] * frequency[None, :]
    cos_part = jnp.cos(angles)[:, None, :]
    sin_part = jnp.sin(angles)[:, None, :]
    leading = vectors[..., :half_size]
    trailing = vectors[..., half_size:]
    return jnp.concatenate([leading * cos_part - trailing * sin_part, trailing * cos_part + leading * sin_part], axis=-1)

def reference(hidden_in, norm_gain, query_proj, kv_proj, prompt_lengths, cache_slot):
    total_tokens = hidden_in.shape[0]
    token_index = jnp.arange(total_tokens, dtype=jnp.int32)
    segment, places = token_places(prompt_lengths, token_index)
    widened = hidden_in.astype(jnp.float32)
    mean_square = lax.optimization_barrier(jnp.mean(widened * widened, axis=1, keepdims=True))
    normed = (widened * lax.rsqrt(mean_square + epsilon) * norm_gain.astype(jnp.float32)[None, :]).astype(jnp.bfloat16)
    contract = (((1,), (1,)), ((), ()))
    query_raw = lax.dot_general(normed, query_proj, contract, preferred_element_type=jnp.float32).reshape(total_tokens, H, HD)
    kv_raw = lax.dot_general(normed, kv_proj, contract, preferred_element_type=jnp.float32).reshape(total_tokens, KVH, 2, HD)
    queries = rotate(query_raw, places).astype(jnp.bfloat16)
    keys = rotate(kv_raw[:, :, 0, :], places).astype(jnp.bfloat16)
    values = kv_raw[:, :, 1, :].astype(jnp.bfloat16)
    group_size = H // KVH
    block_count = total_tokens // TOK_BLK
    score_scale = 1.0 / math.sqrt(HD)

    def one_item(item):
        group_index, block_index = item
        begin = (block_index * TOK_BLK).astype(jnp.int32)
        query_rows = lax.dynamic_slice(queries, (begin, (group_index * group_size).astype(jnp.int32), jnp.int32(0)), (TOK_BLK, group_size, HD))
        key_rows = lax.dynamic_index_in_dim(keys, group_index, 1, keepdims=False)
        value_rows = lax.dynamic_index_in_dim(values, group_index, 1, keepdims=False)
        query_segment = lax.dynamic_slice_in_dim(segment, begin, TOK_BLK, 0)
        query_index = begin + jnp.arange(TOK_BLK, dtype=jnp.int32)
        allowed = (segment[None, :] == query_segment[:, None]) & (token_index[None, :] <= query_index[:, None])
        scores = jnp.einsum('qhd,kd->hqk', query_rows.astype(jnp.float32), key_rows.astype(jnp.float32)) * score_scale
        scores = jnp.where(allowed[None], scores, masked_out)
        row_max = lax.optimization_barrier(jnp.max(scores, axis=2, keepdims=True))
        weights = jnp.where(allowed[None], jnp.exp(scores - row_max), 0.0)
        totals = lax.optimization_barrier(jnp.sum(weights, axis=2))
        rounded = lax.optimization_barrier(weights.astype(jnp.bfloat16)).astype(jnp.float32)
        mixed = jnp.einsum('hqk,kd->hqd', rounded, value_rows.astype(jnp.float32))
        return (mixed / totals[..., None]).astype(jnp.bfloat16)
    groups = jnp.repeat(jnp.arange(KVH, dtype=jnp.int32), block_count)
    blocks = jnp.tile(jnp.arange(block_count, dtype=jnp.int32), KVH)
    outputs = lax.map(one_item, (groups, blocks))
    attention = outputs.reshape(KVH, block_count, group_size, TOK_BLK, HD).transpose(1, 3, 0, 2, 4).reshape(total_tokens, H * HD)
    pages = jnp.stack([keys, values], axis=2).reshape(PAGES, PAGE, 2 * KVH * HD)
    kv_cache = jnp.zeros_like(pages).at[cache_slot].set(pages)
    return (attention, kv_cache)
```

```python
import math

import jax
import jax.numpy as jnp
from jax import lax
from jax.sharding import PartitionSpec as P

D = 4096
H = 32
KVH = 4
HD = 128
PAGES_DEV = 16
MOST = 4096


epsilon = 1e-06
rope_base = 5000000.0
masked_out = -1e30


def token_places(prompt_lengths, token_index):
    prompt_ends = jnp.cumsum(prompt_lengths)
    prompt_starts = prompt_ends - prompt_lengths
    segment = jnp.sum((token_index[:, None] >= prompt_ends[None, :]).astype(jnp.int32), axis=1)
    chosen = segment[:, None] == jnp.arange(prompt_lengths.shape[0], dtype=jnp.int32)[None, :]
    opening = jnp.sum(jnp.where(chosen, prompt_starts[None, :], 0), axis=1)
    return (segment, token_index - opening)


def rotate(vectors, places):
    half_size = vectors.shape[-1] // 2
    frequency = rope_base ** (-(jnp.arange(half_size, dtype=jnp.float32) * 2.0) / vectors.shape[-1])
    angles = places.astype(jnp.float32)[:, None] * frequency[None, :]
    cos_part = jnp.cos(angles)[:, None, :]
    sin_part = jnp.sin(angles)[:, None, :]
    leading = vectors[..., :half_size]
    trailing = vectors[..., half_size:]
    return jnp.concatenate(
        [leading * cos_part - trailing * sin_part, trailing * cos_part + leading * sin_part],
        axis=-1,
    )


def local(hidden_in, norm_gain, query_proj, kv_proj, prompt_lengths, cache_slot):
    count_gx = lax.axis_size("gx")
    count_gy = lax.axis_size("gy")
    where_gx = lax.axis_index("gx")
    where_gy = lax.axis_index("gy")
    local_rows, local_feats = hidden_in.shape
    features = local_feats * count_gy
    block_tokens = local_rows * count_gx // count_gy
    all_tokens = block_tokens * count_gy
    blocks_per_slab = local_rows // block_tokens
    sub = block_tokens // count_gy
    heads_here = query_proj.shape[0] // HD
    query_cols = heads_here * HD
    is_key = where_gx % 2 == 0

    kv_rows = lax.dynamic_slice_in_dim(kv_proj, where_gx * HD, HD, 0)
    stacked = jnp.concatenate([query_proj, kv_rows], axis=0)
    weights_full = lax.all_gather(stacked, "gy", axis=1, tiled=True)
    gain_full = lax.all_gather(norm_gain, "gy", axis=0, tiled=True)

    pieces = hidden_in.reshape(blocks_per_slab, count_gy, sub, local_feats)
    pieces = lax.all_to_all(pieces, "gy", 1, 1, tiled=True)
    rows_here = lax.all_gather(pieces, "gx", axis=0, tiled=False)
    rows_here = rows_here.transpose(0, 1, 3, 2, 4).reshape(block_tokens, features)
    widened = rows_here.astype(jnp.float32)
    squares = jnp.sum(widened * widened, axis=1)
    normed = (
        widened * lax.rsqrt(squares / features + epsilon)[:, None]
        * gain_full.astype(jnp.float32)[None, :]
    ).astype(jnp.bfloat16)
    contract = (((1,), (1,)), ((), ()))
    projected = lax.dot_general(normed, weights_full, contract, preferred_element_type=jnp.float32)

    order = jnp.arange(block_tokens, dtype=jnp.int32)
    my_tokens = (order // sub) * block_tokens + where_gy * sub + order % sub
    unused_segment, my_places = token_places(prompt_lengths, my_tokens)
    queries = rotate(
        projected[:, :query_cols].reshape(block_tokens, heads_here, HD), my_places
    ).astype(jnp.bfloat16)
    half_raw = projected[:, query_cols:]
    rotated = rotate(half_raw[:, None, :], my_places)[:, 0, :]
    mine = jnp.where(is_key, rotated, half_raw).astype(jnp.bfloat16)

    queries = lax.all_to_all(
        queries.reshape(count_gy, sub, query_cols), "gy", 0, 0, tiled=True
    ).reshape(block_tokens, heads_here, HD)
    mine_all = lax.all_gather(mine.reshape(count_gy, sub, HD), "gy", axis=0, tiled=False)
    mine_all = mine_all.transpose(1, 0, 2, 3).reshape(all_tokens, HD)
    other_all = lax.ppermute(mine_all, "gx", [(p, p ^ 1) for p in range(count_gx)])
    keys = jnp.where(is_key, mine_all, other_all)
    values = jnp.where(is_key, other_all, mine_all)

    every_index = jnp.arange(all_tokens, dtype=jnp.int32)
    segment_all, unused_places = token_places(prompt_lengths, every_index)
    first_query = where_gy * block_tokens
    token_index = first_query + order
    segment_own = lax.dynamic_slice_in_dim(segment_all, first_query, block_tokens, 0)
    window_blocks = min(count_gy, MOST // block_tokens + 1)
    window = window_blocks * block_tokens
    window_start = jnp.clip(where_gy - (window_blocks - 1), 0, count_gy - window_blocks) * block_tokens
    key_rows = lax.dynamic_slice_in_dim(keys, window_start, window, 0)
    value_rows = lax.dynamic_slice_in_dim(values, window_start, window, 0)
    key_segment = lax.dynamic_slice_in_dim(segment_all, window_start, window, 0)
    key_index = window_start + jnp.arange(window, dtype=jnp.int32)
    allowed = (key_segment[None, :] == segment_own[:, None]) & (
        key_index[None, :] <= token_index[:, None]
    )
    score_scale = 1.0 / math.sqrt(HD)
    scores = (
        jnp.einsum("qhd,kd->hqk", queries, key_rows, preferred_element_type=jnp.float32)
        * score_scale
    )
    scores = jnp.where(allowed[None], scores, masked_out)
    row_max = jnp.max(scores, axis=2, keepdims=True)
    weights = jnp.where(allowed[None], jnp.exp(scores - row_max), 0.0)
    totals = jnp.sum(weights, axis=2)
    mixed = jnp.einsum(
        "hqk,kd->hqd", weights.astype(jnp.bfloat16), value_rows, preferred_element_type=jnp.float32
    )
    attention = (
        (mixed / totals[..., None])
        .astype(jnp.bfloat16)
        .transpose(1, 0, 2)
        .reshape(block_tokens, query_cols)
    )

    cache_cols = lax.dynamic_slice_in_dim(mine_all, first_query, block_tokens, 0)
    pages_dev = PAGES_DEV
    page_len = block_tokens // pages_dev
    page_range = jnp.arange(pages_dev, dtype=jnp.int32)
    width_cols = cache_cols.shape[1]
    my_pages = cache_cols.reshape(pages_dev, page_len * width_cols)
    capacity = max(1, pages_dev // count_gy)
    slots_all = count_gy * capacity
    owners = (cache_slot // pages_dev).reshape(count_gy, pages_dev)
    earlier = page_range[None, :] < page_range[:, None]
    same_owner = owners[:, :, None] == owners[:, None, :]
    ranks = jnp.sum((same_owner & earlier[None]).astype(jnp.int32), axis=2)
    my_owner = lax.dynamic_index_in_dim(owners, where_gy, 0, keepdims=False)
    my_rank = lax.dynamic_index_in_dim(ranks, where_gy, 0, keepdims=False)
    target = my_owner * capacity + my_rank
    slot_range = jnp.arange(slots_all, dtype=jnp.int32)
    send_map = (slot_range[:, None] == target[None, :]).astype(jnp.bfloat16)
    outgoing = jnp.dot(send_map, my_pages, preferred_element_type=jnp.float32).astype(jnp.bfloat16)
    incoming = lax.all_to_all(outgoing, "gy", split_axis=0, concat_axis=0, tiled=True)
    wanted = where_gy * pages_dev + page_range
    matches = cache_slot[None, :] == wanted[:, None]
    page_ids = jnp.arange(cache_slot.shape[0], dtype=jnp.int32)
    source_page = jnp.sum(jnp.where(matches, page_ids[None, :], 0), axis=1)
    source_rank = jnp.sum(jnp.where(matches, ranks.reshape(-1)[None, :], 0), axis=1)
    source_slot = source_page // pages_dev * capacity + source_rank
    take_map = (source_slot[:, None] == slot_range[None, :]).astype(jnp.bfloat16)
    cache_block = jnp.dot(take_map, incoming, preferred_element_type=jnp.float32)
    cache_block = cache_block.astype(jnp.bfloat16).reshape(pages_dev, page_len, width_cols)
    return (attention, cache_block)


def solution(mesh):
    return jax.shard_map(
        local,
        mesh=mesh,
        in_specs=(P("gx", "gy"), P("gy"), P("gx", "gy"), P(None, "gy"), P(), P()),
        out_specs=(P("gy", "gx"), P("gy", None, "gx")),
        check_vma=False,
    )
```

```python
import math

import jax
import jax.numpy as jnp
from jax import lax
from jax.sharding import PartitionSpec as P

D = 4096
H = 32
KVH = 4
HD = 128
PAGES_DEV = 16
MOST = 4096


epsilon = 1e-06
rope_base = 5000000.0
masked_out = -1e30


def token_places(prompt_lengths, token_index):
    prompt_ends = jnp.cumsum(prompt_lengths)
    prompt_starts = prompt_ends - prompt_lengths
    segment = jnp.sum((token_index[:, None] >= prompt_ends[None, :]).astype(jnp.int32), axis=1)
    chosen = segment[:, None] == jnp.arange(prompt_lengths.shape[0], dtype=jnp.int32)[None, :]
    opening = jnp.sum(jnp.where(chosen, prompt_starts[None, :], 0), axis=1)
    return (segment, token_index - opening)


def rotate(vectors, places):
    half_size = vectors.shape[-1] // 2
    frequency = rope_base ** (-(jnp.arange(half_size, dtype=jnp.float32) * 2.0) / vectors.shape[-1])
    angles = places.astype(jnp.float32)[:, None] * frequency[None, :]
    cos_part = jnp.cos(angles)[:, None, :]
    sin_part = jnp.sin(angles)[:, None, :]
    leading = vectors[..., :half_size]
    trailing = vectors[..., half_size:]
    return jnp.concatenate(
        [leading * cos_part - trailing * sin_part, trailing * cos_part + leading * sin_part],
        axis=-1,
    )


def local(hidden_in, norm_gain, query_proj, kv_proj, prompt_lengths, cache_slot):
    count_gx = lax.axis_size("gx")
    count_gy = lax.axis_size("gy")
    where_gx = lax.axis_index("gx")
    where_gy = lax.axis_index("gy")
    local_rows, local_feats = hidden_in.shape
    features = local_feats * count_gy
    block_tokens = local_rows * count_gx // count_gy
    all_tokens = block_tokens * count_gy
    blocks_per_slab = local_rows // block_tokens
    sub = block_tokens // count_gy
    heads_here = query_proj.shape[0] // HD
    query_cols = heads_here * HD
    is_key = where_gx % 2 == 0

    kv_rows = lax.dynamic_slice_in_dim(kv_proj, where_gx * HD, HD, 0)
    gain_rows = jnp.concatenate(
        [norm_gain[None, :], jnp.zeros((7, local_feats), norm_gain.dtype)], axis=0
    )
    stacked = jnp.concatenate([query_proj, kv_rows, gain_rows], axis=0)
    gathered = lax.all_gather(stacked, "gy", axis=1, tiled=True)
    weight_rows = query_cols + HD
    weights_full = gathered[:weight_rows]
    gain_full = gathered[weight_rows]

    pieces = hidden_in.reshape(blocks_per_slab, count_gy, sub, local_feats)
    pieces = lax.all_to_all(pieces, "gy", 1, 1, tiled=True)
    spread = jnp.broadcast_to(pieces[None], (count_gx,) + pieces.shape)
    rows_here = lax.all_to_all(spread, "gx", 0, 0, tiled=True)
    rows_here = rows_here.transpose(0, 1, 3, 2, 4).reshape(block_tokens, features)
    widened = rows_here.astype(jnp.float32)
    squares = jnp.sum(widened * widened, axis=1)
    normed = (
        widened * lax.rsqrt(squares / features + epsilon)[:, None]
        * gain_full.astype(jnp.float32)[None, :]
    ).astype(jnp.bfloat16)
    contract = (((1,), (1,)), ((), ()))
    projected = lax.dot_general(normed, weights_full, contract, preferred_element_type=jnp.float32)

    order = jnp.arange(block_tokens, dtype=jnp.int32)
    my_tokens = (order // sub) * block_tokens + where_gy * sub + order % sub
    unused_segment, my_places = token_places(prompt_lengths, my_tokens)
    queries = rotate(
        projected[:, :query_cols].reshape(block_tokens, heads_here, HD), my_places
    ).astype(jnp.bfloat16)
    half_raw = projected[:, query_cols:]
    rotated = rotate(half_raw[:, None, :], my_places)[:, 0, :]
    mine = jnp.where(is_key, rotated, half_raw).astype(jnp.bfloat16)

    other = lax.ppermute(mine, "gx", [(p, p ^ 1) for p in range(count_gx)])
    both = jnp.concatenate(
        [jnp.where(is_key, mine, other), jnp.where(is_key, other, mine)], axis=1
    ).reshape(count_gy, sub, 2 * HD)
    window_blocks = min(count_gy, MOST // block_tokens + 1)
    window = window_blocks * block_tokens
    first_blocks = [min(max(b - (window_blocks - 1), 0), count_gy - window_blocks) for b in range(count_gy)]
    chosen = jnp.asarray(
        [[f + w for w in range(window_blocks)] for f in first_blocks], dtype=jnp.int32
    )
    kv_parcel = jnp.take(both, chosen, axis=0).reshape(count_gy, window_blocks * sub * 2 * HD)
    q_parcel = queries.reshape(count_gy, sub * query_cols)
    parcel = jnp.concatenate([q_parcel, kv_parcel], axis=1)
    arrived = lax.all_to_all(parcel, "gy", 0, 0, tiled=True)
    queries = arrived[:, : sub * query_cols].reshape(block_tokens, heads_here, HD)
    kv_rows_all = (
        arrived[:, sub * query_cols :]
        .reshape(count_gy, window_blocks, sub, 2 * HD)
        .transpose(1, 0, 2, 3)
        .reshape(window, 2 * HD)
    )
    key_rows = kv_rows_all[:, :HD]
    value_rows = kv_rows_all[:, HD:]

    every_index = jnp.arange(all_tokens, dtype=jnp.int32)
    segment_all, unused_places = token_places(prompt_lengths, every_index)
    first_query = where_gy * block_tokens
    token_index = first_query + order
    segment_own = lax.dynamic_slice_in_dim(segment_all, first_query, block_tokens, 0)
    window_start = jnp.clip(where_gy - (window_blocks - 1), 0, count_gy - window_blocks) * block_tokens
    key_segment = lax.dynamic_slice_in_dim(segment_all, window_start, window, 0)
    key_index = window_start + jnp.arange(window, dtype=jnp.int32)
    allowed = (key_segment[None, :] == segment_own[:, None]) & (
        key_index[None, :] <= token_index[:, None]
    )
    score_scale = 1.0 / math.sqrt(HD)
    scores = (
        jnp.einsum("qhd,kd->hqk", queries, key_rows, preferred_element_type=jnp.float32)
        * score_scale
    )
    scores = jnp.where(allowed[None], scores, masked_out)
    row_max = jnp.max(scores, axis=2, keepdims=True)
    weights = jnp.where(allowed[None], jnp.exp(scores - row_max), 0.0)
    totals = jnp.sum(weights, axis=2)
    mixed = jnp.einsum(
        "hqk,kd->hqd", weights.astype(jnp.bfloat16), value_rows, preferred_element_type=jnp.float32
    )
    attention = (
        (mixed / totals[..., None])
        .astype(jnp.bfloat16)
        .transpose(1, 0, 2)
        .reshape(block_tokens, query_cols)
    )

    own_block = lax.dynamic_slice_in_dim(kv_rows_all, first_query - window_start, block_tokens, 0)
    cache_cols = jnp.where(is_key, own_block[:, :HD], own_block[:, HD:])
    pages_dev = PAGES_DEV
    page_len = block_tokens // pages_dev
    page_range = jnp.arange(pages_dev, dtype=jnp.int32)
    width_cols = cache_cols.shape[1]
    my_pages = cache_cols.reshape(pages_dev, page_len * width_cols)
    capacity = max(1, pages_dev // count_gy)
    slots_all = count_gy * capacity
    owners = (cache_slot // pages_dev).reshape(count_gy, pages_dev)
    earlier = page_range[None, :] < page_range[:, None]
    same_owner = owners[:, :, None] == owners[:, None, :]
    ranks = jnp.sum((same_owner & earlier[None]).astype(jnp.int32), axis=2)
    my_owner = lax.dynamic_index_in_dim(owners, where_gy, 0, keepdims=False)
    my_rank = lax.dynamic_index_in_dim(ranks, where_gy, 0, keepdims=False)
    target = my_owner * capacity + my_rank
    slot_range = jnp.arange(slots_all, dtype=jnp.int32)
    send_map = (slot_range[:, None] == target[None, :]).astype(jnp.bfloat16)
    outgoing = jnp.dot(send_map, my_pages, preferred_element_type=jnp.float32).astype(jnp.bfloat16)
    incoming = lax.all_to_all(outgoing, "gy", split_axis=0, concat_axis=0, tiled=True)
    wanted = where_gy * pages_dev + page_range
    matches = cache_slot[None, :] == wanted[:, None]
    page_ids = jnp.arange(cache_slot.shape[0], dtype=jnp.int32)
    source_page = jnp.sum(jnp.where(matches, page_ids[None, :], 0), axis=1)
    source_rank = jnp.sum(jnp.where(matches, ranks.reshape(-1)[None, :], 0), axis=1)
    source_slot = source_page // pages_dev * capacity + source_rank
    take_map = (source_slot[:, None] == slot_range[None, :]).astype(jnp.bfloat16)
    cache_block = jnp.dot(take_map, incoming, preferred_element_type=jnp.float32)
    cache_block = cache_block.astype(jnp.bfloat16).reshape(pages_dev, page_len, width_cols)
    return (attention, cache_block)


def solution(mesh):
    return jax.shard_map(
        local,
        mesh=mesh,
        in_specs=(P("gx", "gy"), P("gy"), P("gx", "gy"), P(None, "gy"), P(), P()),
        out_specs=(P("gy", "gx"), P("gy", None, "gx")),
        check_vma=False,
    )
```

```python
import math

import jax
import jax.numpy as jnp
from jax import lax
from jax.sharding import PartitionSpec as P

D = 4096
H = 32
KVH = 4
HD = 128
PAGES_DEV = 16
MOST = 4096


epsilon = 1e-06
rope_base = 5000000.0
masked_out = -1e30


def token_places(prompt_lengths, token_index):
    prompt_ends = jnp.cumsum(prompt_lengths)
    prompt_starts = prompt_ends - prompt_lengths
    segment = jnp.sum((token_index[:, None] >= prompt_ends[None, :]).astype(jnp.int32), axis=1)
    chosen = segment[:, None] == jnp.arange(prompt_lengths.shape[0], dtype=jnp.int32)[None, :]
    opening = jnp.sum(jnp.where(chosen, prompt_starts[None, :], 0), axis=1)
    return (segment, token_index - opening)


def rotate(vectors, places):
    half_size = vectors.shape[-1] // 2
    frequency = rope_base ** (-(jnp.arange(half_size, dtype=jnp.float32) * 2.0) / vectors.shape[-1])
    angles = places.astype(jnp.float32)[:, None] * frequency[None, :]
    cos_part = jnp.cos(angles)[:, None, :]
    sin_part = jnp.sin(angles)[:, None, :]
    leading = vectors[..., :half_size]
    trailing = vectors[..., half_size:]
    return jnp.concatenate(
        [leading * cos_part - trailing * sin_part, trailing * cos_part + leading * sin_part],
        axis=-1,
    )


def local(hidden_in, norm_gain, query_proj, kv_proj, prompt_lengths, cache_slot):
    count_gx = lax.axis_size("gx")
    count_gy = lax.axis_size("gy")
    where_gx = lax.axis_index("gx")
    where_gy = lax.axis_index("gy")
    local_rows, local_feats = hidden_in.shape
    features = local_feats * count_gy
    block_tokens = local_rows * count_gx // count_gy
    all_tokens = block_tokens * count_gy
    blocks_per_slab = local_rows // block_tokens
    sub = block_tokens // count_gy
    heads_here = query_proj.shape[0] // HD
    query_cols = heads_here * HD
    is_key = where_gx % 2 == 0

    kv_rows = lax.dynamic_slice_in_dim(kv_proj, where_gx * HD, HD, 0)
    gain_rows = jnp.concatenate(
        [norm_gain[None, :], jnp.zeros((7, local_feats), norm_gain.dtype)], axis=0
    )
    stacked = jnp.concatenate([query_proj, kv_rows, gain_rows], axis=0)
    gathered = lax.all_gather(stacked, "gy", axis=1, tiled=True)
    weight_rows = query_cols + HD
    weights_full = gathered[:weight_rows]
    gain_full = gathered[weight_rows]

    pieces = hidden_in.reshape(blocks_per_slab, count_gy, sub, local_feats)
    pieces = lax.all_to_all(pieces, "gy", 1, 1, tiled=True)
    spread = jnp.broadcast_to(pieces[None], (count_gx,) + pieces.shape)
    rows_here = lax.all_to_all(spread, "gx", 0, 0, tiled=True)
    rows_here = rows_here.transpose(0, 1, 3, 2, 4).reshape(block_tokens, features)
    widened = rows_here.astype(jnp.float32)
    squares = jnp.sum(widened * widened, axis=1)
    normed = (
        widened * lax.rsqrt(squares / features + epsilon)[:, None]
        * gain_full.astype(jnp.float32)[None, :]
    ).astype(jnp.bfloat16)
    contract = (((1,), (1,)), ((), ()))
    projected = lax.dot_general(normed, weights_full, contract, preferred_element_type=jnp.float32)

    order = jnp.arange(block_tokens, dtype=jnp.int32)
    my_tokens = (order // sub) * block_tokens + where_gy * sub + order % sub
    unused_segment, my_places = token_places(prompt_lengths, my_tokens)
    queries = rotate(
        projected[:, :query_cols].reshape(block_tokens, heads_here, HD), my_places
    ).astype(jnp.bfloat16)
    half_raw = projected[:, query_cols:]
    rotated = rotate(half_raw[:, None, :], my_places)[:, 0, :]
    mine = jnp.where(is_key, rotated, half_raw).astype(jnp.bfloat16)

    window_blocks = min(count_gy, MOST // block_tokens + 1)
    window = window_blocks * block_tokens
    first_blocks = [min(max(b - (window_blocks - 1), 0), count_gy - window_blocks) for b in range(count_gy)]
    chosen = jnp.asarray(
        [[f + w for w in range(window_blocks)] for f in first_blocks], dtype=jnp.int32
    )
    strided = mine.reshape(count_gy, sub, HD)
    kv_parcel = jnp.take(strided, chosen, axis=0).reshape(count_gy, window_blocks * sub * HD)
    q_parcel = queries.reshape(count_gy, sub * query_cols)
    parcel = jnp.concatenate([q_parcel, kv_parcel], axis=1)
    arrived = lax.all_to_all(parcel, "gy", 0, 0, tiled=True)
    queries = arrived[:, : sub * query_cols].reshape(block_tokens, heads_here, HD)
    mine_window = arrived[:, sub * query_cols :].reshape(count_gy, window_blocks, sub, HD)
    other_window = lax.ppermute(mine_window, "gx", [(p, p ^ 1) for p in range(count_gx)])
    key_rows = jnp.where(is_key, mine_window, other_window).reshape(window, HD)
    value_rows = jnp.where(is_key, other_window, mine_window).reshape(window, HD)

    first_query = where_gy * block_tokens
    token_index = first_query + order
    segment_own, unused_places = token_places(prompt_lengths, token_index)
    window_first = jnp.clip(where_gy - (window_blocks - 1), 0, count_gy - window_blocks)
    source_range = jnp.arange(count_gy, dtype=jnp.int32)[:, None, None]
    block_range = jnp.arange(window_blocks, dtype=jnp.int32)[None, :, None]
    sub_range = jnp.arange(sub, dtype=jnp.int32)[None, None, :]
    key_index = (
        (window_first + block_range) * block_tokens + source_range * sub + sub_range
    ).reshape(window)
    key_segment, unused_places = token_places(prompt_lengths, key_index)
    allowed = (key_segment[None, :] == segment_own[:, None]) & (
        key_index[None, :] <= token_index[:, None]
    )
    score_scale = 1.0 / math.sqrt(HD)
    scores = (
        jnp.einsum("qhd,kd->hqk", queries, key_rows, preferred_element_type=jnp.float32)
        * score_scale
    )
    scores = jnp.where(allowed[None], scores, masked_out)
    row_max = jnp.max(scores, axis=2, keepdims=True)
    weights = jnp.where(allowed[None], jnp.exp(scores - row_max), 0.0)
    totals = jnp.sum(weights, axis=2)
    mixed = jnp.einsum(
        "hqk,kd->hqd", weights.astype(jnp.bfloat16), value_rows, preferred_element_type=jnp.float32
    )
    attention = (
        (mixed / totals[..., None])
        .astype(jnp.bfloat16)
        .transpose(1, 0, 2)
        .reshape(block_tokens, query_cols)
    )

    cache_cols = lax.dynamic_index_in_dim(
        mine_window, where_gy - window_first, 1, keepdims=False
    ).reshape(block_tokens, HD)
    pages_dev = PAGES_DEV
    page_len = block_tokens // pages_dev
    page_range = jnp.arange(pages_dev, dtype=jnp.int32)
    width_cols = cache_cols.shape[1]
    my_pages = cache_cols.reshape(pages_dev, page_len * width_cols)
    capacity = max(1, pages_dev // count_gy)
    slots_all = count_gy * capacity
    owners = (cache_slot // pages_dev).reshape(count_gy, pages_dev)
    earlier = page_range[None, :] < page_range[:, None]
    same_owner = owners[:, :, None] == owners[:, None, :]
    ranks = jnp.sum((same_owner & earlier[None]).astype(jnp.int32), axis=2)
    my_owner = lax.dynamic_index_in_dim(owners, where_gy, 0, keepdims=False)
    my_rank = lax.dynamic_index_in_dim(ranks, where_gy, 0, keepdims=False)
    target = my_owner * capacity + my_rank
    slot_range = jnp.arange(slots_all, dtype=jnp.int32)
    send_map = (slot_range[:, None] == target[None, :]).astype(jnp.bfloat16)
    outgoing = jnp.dot(send_map, my_pages, preferred_element_type=jnp.float32).astype(jnp.bfloat16)
    incoming = lax.all_to_all(outgoing, "gy", split_axis=0, concat_axis=0, tiled=True)
    wanted = where_gy * pages_dev + page_range
    matches = cache_slot[None, :] == wanted[:, None]
    page_ids = jnp.arange(cache_slot.shape[0], dtype=jnp.int32)
    source_page = jnp.sum(jnp.where(matches, page_ids[None, :], 0), axis=1)
    source_rank = jnp.sum(jnp.where(matches, ranks.reshape(-1)[None, :], 0), axis=1)
    source_slot = source_page // pages_dev * capacity + source_rank
    take_map = (source_slot[:, None] == slot_range[None, :]).astype(jnp.bfloat16)
    cache_block = jnp.dot(take_map, incoming, preferred_element_type=jnp.float32)
    cache_block = cache_block.astype(jnp.bfloat16).reshape(pages_dev, page_len, width_cols)
    return (attention, cache_block)


def solution(mesh):
    return jax.shard_map(
        local,
        mesh=mesh,
        in_specs=(P("gx", "gy"), P("gy"), P("gx", "gy"), P(None, "gy"), P(), P()),
        out_specs=(P("gy", "gx"), P("gy", None, "gx")),
        check_vma=False,
    )
```

```python
import functools
import math

import jax
import jax.numpy as jnp
from jax import lax
from jax.experimental import pallas as pl
from jax.sharding import PartitionSpec as P

D = 4096
H = 32
KVH = 4
HD = 128
PAGES_DEV = 16
MOST = 4096


epsilon = 1e-06
rope_base = 5000000.0
masked_out = -1e30


def token_places(prompt_lengths, token_index):
    prompt_ends = jnp.cumsum(prompt_lengths)
    prompt_starts = prompt_ends - prompt_lengths
    segment = jnp.sum((token_index[:, None] >= prompt_ends[None, :]).astype(jnp.int32), axis=1)
    chosen = segment[:, None] == jnp.arange(prompt_lengths.shape[0], dtype=jnp.int32)[None, :]
    opening = jnp.sum(jnp.where(chosen, prompt_starts[None, :], 0), axis=1)
    return (segment, token_index - opening)


def rotate(vectors, places):
    half_size = vectors.shape[-1] // 2
    frequency = rope_base ** (-(jnp.arange(half_size, dtype=jnp.float32) * 2.0) / vectors.shape[-1])
    angles = places.astype(jnp.float32)[:, None] * frequency[None, :]
    cos_part = jnp.cos(angles)[:, None, :]
    sin_part = jnp.sin(angles)[:, None, :]
    leading = vectors[..., :half_size]
    trailing = vectors[..., half_size:]
    return jnp.concatenate(
        [leading * cos_part - trailing * sin_part, trailing * cos_part + leading * sin_part],
        axis=-1,
    )


def attention_body(scale, q_ref, k_ref, v_ref, qseg_ref, qidx_ref, kseg_ref, kidx_ref, o_ref):
    scores = lax.dot_general(
        q_ref[...], k_ref[...], (((1,), (1,)), ((), ())), preferred_element_type=jnp.float32
    ) * scale
    allowed = (kseg_ref[...] == qseg_ref[...]) & (kidx_ref[...] <= qidx_ref[...])
    scores = jnp.where(allowed, scores, masked_out)
    row_max = jnp.max(scores, axis=1, keepdims=True)
    weights = jnp.where(allowed, jnp.exp(scores - row_max), 0.0)
    totals = jnp.sum(weights, axis=1, keepdims=True)
    mixed = jnp.dot(weights.astype(jnp.bfloat16), v_ref[...], preferred_element_type=jnp.float32)
    o_ref[...] = (mixed / totals).astype(o_ref.dtype)


def segment_attention(queries, key_rows, value_rows, q_segment, q_index, k_segment, k_index, head_size, row_chunk=64):
    tokens, cols = queries.shape
    heads = cols // head_size
    window = key_rows.shape[0]
    chunks = tokens // row_chunk
    flops = 4 * tokens * window * head_size * heads
    return pl.pallas_call(
        functools.partial(attention_body, 1.0 / math.sqrt(head_size)),
        grid=(heads, chunks),
        in_specs=[
            pl.BlockSpec((row_chunk, head_size), lambda h, r: (r, h)),
            pl.BlockSpec((window, head_size), lambda h, r: (0, 0)),
            pl.BlockSpec((window, head_size), lambda h, r: (0, 0)),
            pl.BlockSpec((row_chunk, 1), lambda h, r: (r, 0)),
            pl.BlockSpec((row_chunk, 1), lambda h, r: (r, 0)),
            pl.BlockSpec((1, window), lambda h, r: (0, 0)),
            pl.BlockSpec((1, window), lambda h, r: (0, 0)),
        ],
        out_specs=pl.BlockSpec((row_chunk, head_size), lambda h, r: (r, h)),
        out_shape=jax.ShapeDtypeStruct((tokens, cols), jnp.bfloat16),
        cost_estimate=pl.CostEstimate(
            flops=flops, transcendentals=tokens * window * heads,
            bytes_accessed=2 * (2 * tokens * cols + 2 * window * head_size) + 8 * (tokens + window),
        ),
    )(queries, key_rows, value_rows, q_segment.reshape(tokens, 1), q_index.reshape(tokens, 1),
      k_segment.reshape(1, window), k_index.reshape(1, window))


def local(hidden_in, norm_gain, query_proj, kv_proj, prompt_lengths, cache_slot):
    count_gx = lax.axis_size("gx")
    count_gy = lax.axis_size("gy")
    where_gx = lax.axis_index("gx")
    where_gy = lax.axis_index("gy")
    local_rows, local_feats = hidden_in.shape
    features = local_feats * count_gy
    block_tokens = local_rows * count_gx // count_gy
    all_tokens = block_tokens * count_gy
    blocks_per_slab = local_rows // block_tokens
    sub = block_tokens // count_gy
    heads_here = query_proj.shape[0] // HD
    query_cols = heads_here * HD
    is_key = where_gx % 2 == 0

    kv_rows = lax.dynamic_slice_in_dim(kv_proj, where_gx * HD, HD, 0)
    gain_rows = jnp.concatenate(
        [norm_gain[None, :], jnp.zeros((7, local_feats), norm_gain.dtype)], axis=0
    )
    stacked = jnp.concatenate([query_proj, kv_rows, gain_rows], axis=0)
    gathered = lax.all_gather(stacked, "gy", axis=1, tiled=True)
    weight_rows = query_cols + HD
    weights_full = gathered[:weight_rows]
    gain_full = gathered[weight_rows]

    pieces = hidden_in.reshape(blocks_per_slab, count_gy, sub, local_feats)
    pieces = lax.all_to_all(pieces, "gy", 1, 1, tiled=True)
    spread = jnp.broadcast_to(pieces[None], (count_gx,) + pieces.shape)
    rows_here = lax.all_to_all(spread, "gx", 0, 0, tiled=True)
    rows_here = rows_here.transpose(0, 1, 3, 2, 4).reshape(block_tokens, features)
    widened = rows_here.astype(jnp.float32)
    squares = jnp.sum(widened * widened, axis=1)
    normed = (
        widened * lax.rsqrt(squares / features + epsilon)[:, None]
        * gain_full.astype(jnp.float32)[None, :]
    ).astype(jnp.bfloat16)
    contract = (((1,), (1,)), ((), ()))
    projected = lax.dot_general(normed, weights_full, contract, preferred_element_type=jnp.float32)

    order = jnp.arange(block_tokens, dtype=jnp.int32)
    my_tokens = (order // sub) * block_tokens + where_gy * sub + order % sub
    unused_segment, my_places = token_places(prompt_lengths, my_tokens)
    queries = rotate(
        projected[:, :query_cols].reshape(block_tokens, heads_here, HD), my_places
    ).astype(jnp.bfloat16)
    half_raw = projected[:, query_cols:]
    rotated = rotate(half_raw[:, None, :], my_places)[:, 0, :]
    mine = jnp.where(is_key, rotated, half_raw).astype(jnp.bfloat16)

    window_blocks = min(count_gy, MOST // block_tokens + 1)
    window = window_blocks * block_tokens
    first_blocks = [min(max(b - (window_blocks - 1), 0), count_gy - window_blocks) for b in range(count_gy)]
    chosen = jnp.asarray(
        [[f + w for w in range(window_blocks)] for f in first_blocks], dtype=jnp.int32
    )
    strided = mine.reshape(count_gy, sub, HD)
    kv_parcel = jnp.take(strided, chosen, axis=0).reshape(count_gy, window_blocks * sub * HD)
    q_parcel = queries.reshape(count_gy, sub * query_cols)
    parcel = jnp.concatenate([q_parcel, kv_parcel], axis=1)
    arrived = lax.all_to_all(parcel, "gy", 0, 0, tiled=True)
    queries = arrived[:, : sub * query_cols].reshape(block_tokens, heads_here, HD)
    mine_window = arrived[:, sub * query_cols :].reshape(count_gy, window_blocks, sub, HD)
    other_window = lax.ppermute(mine_window, "gx", [(p, p ^ 1) for p in range(count_gx)])
    key_rows = jnp.where(is_key, mine_window, other_window).reshape(window, HD)
    value_rows = jnp.where(is_key, other_window, mine_window).reshape(window, HD)

    first_query = where_gy * block_tokens
    token_index = first_query + order
    segment_own, unused_places = token_places(prompt_lengths, token_index)
    window_first = jnp.clip(where_gy - (window_blocks - 1), 0, count_gy - window_blocks)
    source_range = jnp.arange(count_gy, dtype=jnp.int32)[:, None, None]
    block_range = jnp.arange(window_blocks, dtype=jnp.int32)[None, :, None]
    sub_range = jnp.arange(sub, dtype=jnp.int32)[None, None, :]
    key_index = (
        (window_first + block_range) * block_tokens + source_range * sub + sub_range
    ).reshape(window)
    key_segment, unused_places = token_places(prompt_lengths, key_index)
    attention = segment_attention(
        queries.reshape(block_tokens, query_cols), key_rows, value_rows,
        segment_own, token_index, key_segment, key_index, HD,
    )

    cache_cols = lax.dynamic_index_in_dim(
        mine_window, where_gy - window_first, 1, keepdims=False
    ).reshape(block_tokens, HD)
    pages_dev = PAGES_DEV
    page_len = block_tokens // pages_dev
    page_range = jnp.arange(pages_dev, dtype=jnp.int32)
    width_cols = cache_cols.shape[1]
    my_pages = cache_cols.reshape(pages_dev, page_len * width_cols)
    capacity = max(1, pages_dev // count_gy)
    slots_all = count_gy * capacity
    owners = (cache_slot // pages_dev).reshape(count_gy, pages_dev)
    earlier = page_range[None, :] < page_range[:, None]
    same_owner = owners[:, :, None] == owners[:, None, :]
    ranks = jnp.sum((same_owner & earlier[None]).astype(jnp.int32), axis=2)
    my_owner = lax.dynamic_index_in_dim(owners, where_gy, 0, keepdims=False)
    my_rank = lax.dynamic_index_in_dim(ranks, where_gy, 0, keepdims=False)
    target = my_owner * capacity + my_rank
    slot_range = jnp.arange(slots_all, dtype=jnp.int32)
    send_map = (slot_range[:, None] == target[None, :]).astype(jnp.bfloat16)
    outgoing = jnp.dot(send_map, my_pages, preferred_element_type=jnp.float32).astype(jnp.bfloat16)
    incoming = lax.all_to_all(outgoing, "gy", split_axis=0, concat_axis=0, tiled=True)
    wanted = where_gy * pages_dev + page_range
    matches = cache_slot[None, :] == wanted[:, None]
    page_ids = jnp.arange(cache_slot.shape[0], dtype=jnp.int32)
    source_page = jnp.sum(jnp.where(matches, page_ids[None, :], 0), axis=1)
    source_rank = jnp.sum(jnp.where(matches, ranks.reshape(-1)[None, :], 0), axis=1)
    source_slot = source_page // pages_dev * capacity + source_rank
    take_map = (source_slot[:, None] == slot_range[None, :]).astype(jnp.bfloat16)
    cache_block = jnp.dot(take_map, incoming, preferred_element_type=jnp.float32)
    cache_block = cache_block.astype(jnp.bfloat16).reshape(pages_dev, page_len, width_cols)
    return (attention, cache_block)


def solution(mesh):
    return jax.shard_map(
        local,
        mesh=mesh,
        in_specs=(P("gx", "gy"), P("gy"), P("gx", "gy"), P(None, "gy"), P(), P()),
        out_specs=(P("gy", "gx"), P("gy", None, "gx")),
        check_vma=False,
    )
```

```python
import functools
import math

import jax
import jax.numpy as jnp
from jax import lax
from jax.experimental import pallas as pl
from jax.sharding import PartitionSpec as P

D = 4096
H = 32
KVH = 4
HD = 128
PAGES_DEV = 16
MOST = 4096


epsilon = 1e-06
rope_base = 5000000.0
masked_out = -1e30


def token_places(prompt_lengths, token_index):
    prompt_ends = jnp.cumsum(prompt_lengths)
    prompt_starts = prompt_ends - prompt_lengths
    segment = jnp.sum((token_index[:, None] >= prompt_ends[None, :]).astype(jnp.int32), axis=1)
    chosen = segment[:, None] == jnp.arange(prompt_lengths.shape[0], dtype=jnp.int32)[None, :]
    opening = jnp.sum(jnp.where(chosen, prompt_starts[None, :], 0), axis=1)
    return (segment, token_index - opening)


def rotate(vectors, places):
    half_size = vectors.shape[-1] // 2
    frequency = rope_base ** (-(jnp.arange(half_size, dtype=jnp.float32) * 2.0) / vectors.shape[-1])
    angles = places.astype(jnp.float32)[:, None] * frequency[None, :]
    cos_part = jnp.cos(angles)[:, None, :]
    sin_part = jnp.sin(angles)[:, None, :]
    leading = vectors[..., :half_size]
    trailing = vectors[..., half_size:]
    return jnp.concatenate(
        [leading * cos_part - trailing * sin_part, trailing * cos_part + leading * sin_part],
        axis=-1,
    )


def attention_body(scale, heads, head_size, q_ref, k_ref, v_ref, qseg_ref, qidx_ref, kseg_ref, kidx_ref, o_ref):
    allowed = (kseg_ref[...] == qseg_ref[...]) & (kidx_ref[...] <= qidx_ref[...])
    for h in range(heads):
        columns = slice(h * head_size, (h + 1) * head_size)
        scores = lax.dot_general(
            q_ref[:, columns], k_ref[...], (((1,), (1,)), ((), ())),
            preferred_element_type=jnp.float32,
        ) * scale
        scores = jnp.where(allowed, scores, masked_out)
        row_max = jnp.max(scores, axis=1, keepdims=True)
        weights = jnp.exp(scores - row_max)
        totals = jnp.sum(weights, axis=1, keepdims=True)
        mixed = jnp.dot(weights.astype(jnp.bfloat16), v_ref[...], preferred_element_type=jnp.float32)
        o_ref[:, columns] = (mixed / totals).astype(o_ref.dtype)


def segment_attention(queries, key_rows, value_rows, q_segment, q_index, k_segment, k_index, head_size, row_chunk=64):
    tokens, cols = queries.shape
    heads = cols // head_size
    window = key_rows.shape[0]
    flops = 4 * tokens * window * head_size * heads
    return pl.pallas_call(
        functools.partial(attention_body, 1.0 / math.sqrt(head_size), heads, head_size),
        grid=(tokens // row_chunk,),
        in_specs=[
            pl.BlockSpec((row_chunk, cols), lambda r: (r, 0)),
            pl.BlockSpec((window, head_size), lambda r: (0, 0)),
            pl.BlockSpec((window, head_size), lambda r: (0, 0)),
            pl.BlockSpec((row_chunk, 1), lambda r: (r, 0)),
            pl.BlockSpec((row_chunk, 1), lambda r: (r, 0)),
            pl.BlockSpec((1, window), lambda r: (0, 0)),
            pl.BlockSpec((1, window), lambda r: (0, 0)),
        ],
        out_specs=pl.BlockSpec((row_chunk, cols), lambda r: (r, 0)),
        out_shape=jax.ShapeDtypeStruct((tokens, cols), jnp.bfloat16),
        cost_estimate=pl.CostEstimate(
            flops=flops, transcendentals=tokens * window * heads,
            bytes_accessed=2 * (2 * tokens * cols + 2 * window * head_size) + 8 * (tokens + window),
        ),
    )(queries, key_rows, value_rows, q_segment.reshape(tokens, 1), q_index.reshape(tokens, 1),
      k_segment.reshape(1, window), k_index.reshape(1, window))


def local(hidden_in, norm_gain, query_proj, kv_proj, prompt_lengths, cache_slot):
    count_gx = lax.axis_size("gx")
    count_gy = lax.axis_size("gy")
    where_gx = lax.axis_index("gx")
    where_gy = lax.axis_index("gy")
    local_rows, local_feats = hidden_in.shape
    features = local_feats * count_gy
    block_tokens = local_rows * count_gx // count_gy
    all_tokens = block_tokens * count_gy
    blocks_per_slab = local_rows // block_tokens
    sub = block_tokens // count_gy
    heads_here = query_proj.shape[0] // HD
    query_cols = heads_here * HD
    is_key = where_gx % 2 == 0

    kv_rows = lax.dynamic_slice_in_dim(kv_proj, where_gx * HD, HD, 0)
    gain_rows = jnp.concatenate(
        [norm_gain[None, :], jnp.zeros((7, local_feats), norm_gain.dtype)], axis=0
    )
    stacked = jnp.concatenate([query_proj, kv_rows, gain_rows], axis=0)
    gathered = lax.all_gather(stacked, "gy", axis=1, tiled=True)
    weight_rows = query_cols + HD
    weights_full = gathered[:weight_rows]
    gain_full = gathered[weight_rows]

    pieces = hidden_in.reshape(blocks_per_slab, count_gy, sub, local_feats)
    pieces = lax.all_to_all(pieces, "gy", 1, 1, tiled=True)
    spread = jnp.broadcast_to(pieces[None], (count_gx,) + pieces.shape)
    rows_here = lax.all_to_all(spread, "gx", 0, 0, tiled=True)
    rows_here = rows_here.transpose(0, 1, 3, 2, 4).reshape(block_tokens, features)
    widened = rows_here.astype(jnp.float32)
    squares = jnp.sum(widened * widened, axis=1)
    normed = (
        widened * lax.rsqrt(squares / features + epsilon)[:, None]
        * gain_full.astype(jnp.float32)[None, :]
    ).astype(jnp.bfloat16)
    contract = (((1,), (1,)), ((), ()))
    projected = lax.dot_general(normed, weights_full, contract, preferred_element_type=jnp.float32)

    order = jnp.arange(block_tokens, dtype=jnp.int32)
    my_tokens = (order // sub) * block_tokens + where_gy * sub + order % sub
    unused_segment, my_places = token_places(prompt_lengths, my_tokens)
    queries = rotate(
        projected[:, :query_cols].reshape(block_tokens, heads_here, HD), my_places
    ).astype(jnp.bfloat16)
    half_raw = projected[:, query_cols:]
    rotated = rotate(half_raw[:, None, :], my_places)[:, 0, :]
    mine = jnp.where(is_key, rotated, half_raw).astype(jnp.bfloat16)

    needed_blocks = MOST // block_tokens + 1
    window_blocks = min(count_gy, -(-needed_blocks * sub // 16) * 16 // sub)
    window = window_blocks * block_tokens
    first_blocks = [min(max(b - (window_blocks - 1), 0), count_gy - window_blocks) for b in range(count_gy)]
    chosen = jnp.asarray(
        [[f + w for w in range(window_blocks)] for f in first_blocks], dtype=jnp.int32
    )
    strided = mine.reshape(count_gy, sub, HD)
    kv_parcel = jnp.take(strided, chosen, axis=0).reshape(count_gy, window_blocks * sub, HD)
    q_parcel = queries.reshape(count_gy, sub * heads_here, HD)
    parcel = jnp.concatenate([q_parcel, kv_parcel], axis=1)
    arrived = lax.all_to_all(parcel, "gy", 0, 0, tiled=True)
    queries = arrived[:, : sub * heads_here].reshape(block_tokens, query_cols)
    mine_window = arrived[:, sub * heads_here :]
    other_window = lax.ppermute(mine_window, "gx", [(p, p ^ 1) for p in range(count_gx)])
    key_rows = jnp.where(is_key, mine_window, other_window).reshape(window, HD)
    value_rows = jnp.where(is_key, other_window, mine_window).reshape(window, HD)

    first_query = where_gy * block_tokens
    token_index = first_query + order
    segment_own, unused_places = token_places(prompt_lengths, token_index)
    window_first = jnp.clip(where_gy - (window_blocks - 1), 0, count_gy - window_blocks)
    source_range = jnp.arange(count_gy, dtype=jnp.int32)[:, None, None]
    block_range = jnp.arange(window_blocks, dtype=jnp.int32)[None, :, None]
    sub_range = jnp.arange(sub, dtype=jnp.int32)[None, None, :]
    key_index = (
        (window_first + block_range) * block_tokens + source_range * sub + sub_range
    ).reshape(window)
    key_segment, unused_places = token_places(prompt_lengths, key_index)
    attention = segment_attention(
        queries, key_rows, value_rows,
        segment_own, token_index, key_segment, key_index, HD,
    )

    cache_cols = lax.dynamic_index_in_dim(
        mine_window.reshape(count_gy, window_blocks, sub, HD), where_gy - window_first, 1, keepdims=False
    ).reshape(block_tokens, HD)
    pages_dev = PAGES_DEV
    page_len = block_tokens // pages_dev
    page_range = jnp.arange(pages_dev, dtype=jnp.int32)
    width_cols = cache_cols.shape[1]
    my_pages = cache_cols.reshape(pages_dev, page_len * width_cols)
    capacity = max(1, pages_dev // count_gy)
    slots_all = count_gy * capacity
    owners = (cache_slot // pages_dev).reshape(count_gy, pages_dev)
    earlier = page_range[None, :] < page_range[:, None]
    same_owner = owners[:, :, None] == owners[:, None, :]
    ranks = jnp.sum((same_owner & earlier[None]).astype(jnp.int32), axis=2)
    my_owner = lax.dynamic_index_in_dim(owners, where_gy, 0, keepdims=False)
    my_rank = lax.dynamic_index_in_dim(ranks, where_gy, 0, keepdims=False)
    target = my_owner * capacity + my_rank
    slot_range = jnp.arange(slots_all, dtype=jnp.int32)
    send_map = (slot_range[:, None] == target[None, :]).astype(jnp.bfloat16)
    outgoing = jnp.dot(send_map, my_pages, preferred_element_type=jnp.float32).astype(jnp.bfloat16)
    incoming = lax.all_to_all(outgoing, "gy", split_axis=0, concat_axis=0, tiled=True)
    wanted = where_gy * pages_dev + page_range
    matches = cache_slot[None, :] == wanted[:, None]
    page_ids = jnp.arange(cache_slot.shape[0], dtype=jnp.int32)
    source_page = jnp.sum(jnp.where(matches, page_ids[None, :], 0), axis=1)
    source_rank = jnp.sum(jnp.where(matches, ranks.reshape(-1)[None, :], 0), axis=1)
    source_slot = source_page // pages_dev * capacity + source_rank
    take_map = (source_slot[:, None] == slot_range[None, :]).astype(jnp.bfloat16)
    cache_block = jnp.dot(take_map, incoming, preferred_element_type=jnp.float32)
    cache_block = cache_block.astype(jnp.bfloat16).reshape(pages_dev, page_len, width_cols)
    return (attention, cache_block)


def solution(mesh):
    return jax.shard_map(
        local,
        mesh=mesh,
        in_specs=(P("gx", "gy"), P("gy"), P("gx", "gy"), P(None, "gy"), P(), P()),
        out_specs=(P("gy", "gx"), P("gy", None, "gx")),
        check_vma=False,
    )
```

```python
import functools
import math

import jax
import jax.numpy as jnp
from jax import lax
from jax.experimental import pallas as pl
from jax.sharding import PartitionSpec as P

D = 4096
H = 32
KVH = 4
HD = 128
PAGES_DEV = 16
MOST = 4096


epsilon = 1e-06
rope_base = 5000000.0
masked_out = -1e30


def token_places(prompt_lengths, token_index):
    prompt_ends = jnp.cumsum(prompt_lengths)
    prompt_starts = prompt_ends - prompt_lengths
    segment = jnp.sum((token_index[:, None] >= prompt_ends[None, :]).astype(jnp.int32), axis=1)
    chosen = segment[:, None] == jnp.arange(prompt_lengths.shape[0], dtype=jnp.int32)[None, :]
    opening = jnp.sum(jnp.where(chosen, prompt_starts[None, :], 0), axis=1)
    return (segment, token_index - opening)


def rotate(vectors, places):
    half_size = vectors.shape[-1] // 2
    frequency = rope_base ** (-(jnp.arange(half_size, dtype=jnp.float32) * 2.0) / vectors.shape[-1])
    angles = places.astype(jnp.float32)[:, None] * frequency[None, :]
    cos_part = jnp.cos(angles)[:, None, :]
    sin_part = jnp.sin(angles)[:, None, :]
    leading = vectors[..., :half_size]
    trailing = vectors[..., half_size:]
    return jnp.concatenate(
        [leading * cos_part - trailing * sin_part, trailing * cos_part + leading * sin_part],
        axis=-1,
    )


def attention_body(scale, heads, head_size, q_ref, k_ref, v_ref, qseg_ref, qidx_ref, kseg_ref, kidx_ref, o_ref):
    allowed = (kseg_ref[...] == qseg_ref[...]) & (kidx_ref[...] <= qidx_ref[...])
    for h in range(heads):
        columns = slice(h * head_size, (h + 1) * head_size)
        scores = lax.dot_general(
            q_ref[:, columns], k_ref[...], (((1,), (1,)), ((), ())),
            preferred_element_type=jnp.float32,
        ) * scale
        scores = jnp.where(allowed, scores, masked_out)
        row_max = jnp.max(scores, axis=1, keepdims=True)
        weights = jnp.exp(scores - row_max)
        totals = jnp.sum(weights, axis=1, keepdims=True)
        mixed = jnp.dot(weights.astype(jnp.bfloat16), v_ref[...], preferred_element_type=jnp.float32)
        o_ref[:, columns] = (mixed / totals).astype(o_ref.dtype)


def segment_attention(queries, key_rows, value_rows, q_segment, q_index, k_segment, k_index, head_size, row_chunk=64):
    tokens, cols = queries.shape
    heads = cols // head_size
    window = key_rows.shape[0]
    flops = 4 * tokens * window * head_size * heads
    return pl.pallas_call(
        functools.partial(attention_body, 1.0 / math.sqrt(head_size), heads, head_size),
        grid=(tokens // row_chunk,),
        in_specs=[
            pl.BlockSpec((row_chunk, cols), lambda r: (r, 0)),
            pl.BlockSpec((window, head_size), lambda r: (0, 0)),
            pl.BlockSpec((window, head_size), lambda r: (0, 0)),
            pl.BlockSpec((row_chunk, 1), lambda r: (r, 0)),
            pl.BlockSpec((row_chunk, 1), lambda r: (r, 0)),
            pl.BlockSpec((1, window), lambda r: (0, 0)),
            pl.BlockSpec((1, window), lambda r: (0, 0)),
        ],
        out_specs=pl.BlockSpec((row_chunk, cols), lambda r: (r, 0)),
        out_shape=jax.ShapeDtypeStruct((tokens, cols), jnp.bfloat16),
        cost_estimate=pl.CostEstimate(
            flops=flops, transcendentals=tokens * window * heads,
            bytes_accessed=2 * (2 * tokens * cols + 2 * window * head_size) + 8 * (tokens + window),
        ),
    )(queries, key_rows, value_rows, q_segment.reshape(tokens, 1), q_index.reshape(tokens, 1),
      k_segment.reshape(1, window), k_index.reshape(1, window))


def local(hidden_in, norm_gain, query_proj, kv_proj, prompt_lengths, cache_slot):
    count_gx = lax.axis_size("gx")
    count_gy = lax.axis_size("gy")
    where_gx = lax.axis_index("gx")
    where_gy = lax.axis_index("gy")
    local_rows, local_feats = hidden_in.shape
    features = local_feats * count_gy
    block_tokens = local_rows * count_gx // count_gy
    all_tokens = block_tokens * count_gy
    blocks_per_slab = local_rows // block_tokens
    sub = block_tokens // count_gy
    heads_here = query_proj.shape[0] // HD
    query_cols = heads_here * HD
    is_key = where_gx % 2 == 0

    kv_rows = lax.dynamic_slice_in_dim(kv_proj, where_gx * HD, HD, 0)
    gain_rows = jnp.concatenate(
        [norm_gain[None, :], jnp.zeros((7, local_feats), norm_gain.dtype)], axis=0
    )
    kv_stack = jnp.concatenate([kv_rows, gain_rows], axis=0)
    kv_spread = jnp.broadcast_to(kv_stack[None], (count_gy,) + kv_stack.shape)
    kv_arrived = lax.all_to_all(kv_spread, "gy", 0, 0, tiled=True)
    kv_weights = kv_arrived[:, :HD]
    gain_full = kv_arrived[:, HD].reshape(features)
    query_weights = lax.all_gather(query_proj, "gy", axis=1, tiled=True)

    pieces = hidden_in.reshape(blocks_per_slab, count_gy, sub, local_feats)
    pieces = lax.all_to_all(pieces, "gy", 1, 1, tiled=True)
    spread = jnp.broadcast_to(pieces[None], (count_gx,) + pieces.shape)
    rows_here = lax.all_to_all(spread, "gx", 0, 0, tiled=True)
    rows_here = rows_here.transpose(0, 1, 3, 2, 4).reshape(block_tokens, features)
    widened = rows_here.astype(jnp.float32)
    squares = jnp.sum(widened * widened, axis=1)
    normed = (
        widened * lax.rsqrt(squares / features + epsilon)[:, None]
        * gain_full.astype(jnp.float32)[None, :]
    ).astype(jnp.bfloat16)
    contract = (((1,), (1,)), ((), ()))
    half_raw = lax.dot_general(
        normed.reshape(block_tokens, count_gy, local_feats), kv_weights,
        (((1, 2), (0, 2)), ((), ())), preferred_element_type=jnp.float32,
    )

    order = jnp.arange(block_tokens, dtype=jnp.int32)
    my_tokens = (order // sub) * block_tokens + where_gy * sub + order % sub
    unused_segment, my_places = token_places(prompt_lengths, my_tokens)
    rotated = rotate(half_raw[:, None, :], my_places)[:, 0, :]
    mine = jnp.where(is_key, rotated, half_raw).astype(jnp.bfloat16)

    needed_blocks = MOST // block_tokens + 1
    window_blocks = min(count_gy, -(-needed_blocks * sub // 16) * 16 // sub)
    window = window_blocks * block_tokens
    first_blocks = [min(max(b - (window_blocks - 1), 0), count_gy - window_blocks) for b in range(count_gy)]
    chosen = jnp.asarray(
        [[f + w for w in range(window_blocks)] for f in first_blocks], dtype=jnp.int32
    )
    strided = mine.reshape(count_gy, sub, HD)
    kv_parcel = jnp.take(strided, chosen, axis=0).reshape(count_gy, window_blocks * sub, HD)
    mine_window = lax.all_to_all(kv_parcel, "gy", 0, 0, tiled=True)
    projected = lax.dot_general(normed, query_weights, contract, preferred_element_type=jnp.float32)
    queries = rotate(projected.reshape(block_tokens, heads_here, HD), my_places).astype(jnp.bfloat16)
    queries = lax.all_to_all(
        queries.reshape(count_gy, sub * heads_here, HD), "gy", 0, 0, tiled=True
    ).reshape(block_tokens, query_cols)
    other_window = lax.ppermute(mine_window, "gx", [(p, p ^ 1) for p in range(count_gx)])
    key_rows = jnp.where(is_key, mine_window, other_window).reshape(window, HD)
    value_rows = jnp.where(is_key, other_window, mine_window).reshape(window, HD)

    first_query = where_gy * block_tokens
    token_index = first_query + order
    segment_own, unused_places = token_places(prompt_lengths, token_index)
    window_first = jnp.clip(where_gy - (window_blocks - 1), 0, count_gy - window_blocks)
    source_range = jnp.arange(count_gy, dtype=jnp.int32)[:, None, None]
    block_range = jnp.arange(window_blocks, dtype=jnp.int32)[None, :, None]
    sub_range = jnp.arange(sub, dtype=jnp.int32)[None, None, :]
    key_index = (
        (window_first + block_range) * block_tokens + source_range * sub + sub_range
    ).reshape(window)
    key_segment, unused_places = token_places(prompt_lengths, key_index)
    attention = segment_attention(
        queries, key_rows, value_rows,
        segment_own, token_index, key_segment, key_index, HD,
    )

    cache_cols = lax.dynamic_index_in_dim(
        mine_window.reshape(count_gy, window_blocks, sub, HD), where_gy - window_first, 1, keepdims=False
    ).reshape(block_tokens, HD)
    pages_dev = PAGES_DEV
    page_len = block_tokens // pages_dev
    page_range = jnp.arange(pages_dev, dtype=jnp.int32)
    width_cols = cache_cols.shape[1]
    my_pages = cache_cols.reshape(pages_dev, page_len * width_cols)
    capacity = max(1, pages_dev // count_gy)
    slots_all = count_gy * capacity
    owners = (cache_slot // pages_dev).reshape(count_gy, pages_dev)
    earlier = page_range[None, :] < page_range[:, None]
    same_owner = owners[:, :, None] == owners[:, None, :]
    ranks = jnp.sum((same_owner & earlier[None]).astype(jnp.int32), axis=2)
    my_owner = lax.dynamic_index_in_dim(owners, where_gy, 0, keepdims=False)
    my_rank = lax.dynamic_index_in_dim(ranks, where_gy, 0, keepdims=False)
    target = my_owner * capacity + my_rank
    slot_range = jnp.arange(slots_all, dtype=jnp.int32)
    send_map = (slot_range[:, None] == target[None, :]).astype(jnp.bfloat16)
    outgoing = jnp.dot(send_map, my_pages, preferred_element_type=jnp.float32).astype(jnp.bfloat16)
    incoming = lax.all_to_all(outgoing, "gy", split_axis=0, concat_axis=0, tiled=True)
    wanted = where_gy * pages_dev + page_range
    matches = cache_slot[None, :] == wanted[:, None]
    page_ids = jnp.arange(cache_slot.shape[0], dtype=jnp.int32)
    source_page = jnp.sum(jnp.where(matches, page_ids[None, :], 0), axis=1)
    source_rank = jnp.sum(jnp.where(matches, ranks.reshape(-1)[None, :], 0), axis=1)
    source_slot = source_page // pages_dev * capacity + source_rank
    take_map = (source_slot[:, None] == slot_range[None, :]).astype(jnp.bfloat16)
    cache_block = jnp.dot(take_map, incoming, preferred_element_type=jnp.float32)
    cache_block = cache_block.astype(jnp.bfloat16).reshape(pages_dev, page_len, width_cols)
    return (attention, cache_block)


def solution(mesh):
    return jax.shard_map(
        local,
        mesh=mesh,
        in_specs=(P("gx", "gy"), P("gy"), P("gx", "gy"), P(None, "gy"), P(), P()),
        out_specs=(P("gy", "gx"), P("gy", None, "gx")),
        check_vma=False,
    )
```

```python
import functools
import math

import jax
import jax.numpy as jnp
from jax import lax
from jax.experimental import pallas as pl
from jax.sharding import PartitionSpec as P

D = 4096
H = 32
KVH = 4
HD = 128
PAGES_DEV = 16
MOST = 4096


epsilon = 1e-06
rope_base = 5000000.0
masked_out = -1e30
GX = ("x", "core")
GY = ("y", "z")


def token_places(prompt_lengths, token_index):
    prompt_ends = jnp.cumsum(prompt_lengths)
    prompt_starts = prompt_ends - prompt_lengths
    segment = jnp.sum((token_index[:, None] >= prompt_ends[None, :]).astype(jnp.int32), axis=1)
    chosen = segment[:, None] == jnp.arange(prompt_lengths.shape[0], dtype=jnp.int32)[None, :]
    opening = jnp.sum(jnp.where(chosen, prompt_starts[None, :], 0), axis=1)
    return (segment, token_index - opening)


def rotate(vectors, places):
    half_size = vectors.shape[-1] // 2
    frequency = rope_base ** (-(jnp.arange(half_size, dtype=jnp.float32) * 2.0) / vectors.shape[-1])
    angles = places.astype(jnp.float32)[:, None] * frequency[None, :]
    cos_part = jnp.cos(angles)[:, None, :]
    sin_part = jnp.sin(angles)[:, None, :]
    leading = vectors[..., :half_size]
    trailing = vectors[..., half_size:]
    return jnp.concatenate(
        [leading * cos_part - trailing * sin_part, trailing * cos_part + leading * sin_part],
        axis=-1,
    )


def attention_body(scale, heads, head_size, q_ref, k_ref, v_ref, qseg_ref, qidx_ref, kseg_ref, kidx_ref, o_ref):
    allowed = (kseg_ref[...] == qseg_ref[...]) & (kidx_ref[...] <= qidx_ref[...])
    for h in range(heads):
        columns = slice(h * head_size, (h + 1) * head_size)
        scores = lax.dot_general(
            q_ref[:, columns], k_ref[...], (((1,), (1,)), ((), ())),
            preferred_element_type=jnp.float32,
        ) * scale
        scores = jnp.where(allowed, scores, masked_out)
        row_max = jnp.max(scores, axis=1, keepdims=True)
        weights = jnp.exp(scores - row_max)
        totals = jnp.sum(weights, axis=1, keepdims=True)
        mixed = jnp.dot(weights.astype(jnp.bfloat16), v_ref[...], preferred_element_type=jnp.float32)
        o_ref[:, columns] = (mixed / totals).astype(o_ref.dtype)


def segment_attention(queries, key_rows, value_rows, q_segment, q_index, k_segment, k_index, head_size, row_chunk=64):
    tokens, cols = queries.shape
    heads = cols // head_size
    window = key_rows.shape[0]
    flops = 4 * tokens * window * head_size * heads
    return pl.pallas_call(
        functools.partial(attention_body, 1.0 / math.sqrt(head_size), heads, head_size),
        grid=(tokens // row_chunk,),
        in_specs=[
            pl.BlockSpec((row_chunk, cols), lambda r: (r, 0)),
            pl.BlockSpec((window, head_size), lambda r: (0, 0)),
            pl.BlockSpec((window, head_size), lambda r: (0, 0)),
            pl.BlockSpec((row_chunk, 1), lambda r: (r, 0)),
            pl.BlockSpec((row_chunk, 1), lambda r: (r, 0)),
            pl.BlockSpec((1, window), lambda r: (0, 0)),
            pl.BlockSpec((1, window), lambda r: (0, 0)),
        ],
        out_specs=pl.BlockSpec((row_chunk, cols), lambda r: (r, 0)),
        out_shape=jax.ShapeDtypeStruct((tokens, cols), jnp.bfloat16),
        cost_estimate=pl.CostEstimate(
            flops=flops, transcendentals=tokens * window * heads,
            bytes_accessed=2 * (2 * tokens * cols + 2 * window * head_size) + 8 * (tokens + window),
        ),
    )(queries, key_rows, value_rows, q_segment.reshape(tokens, 1), q_index.reshape(tokens, 1),
      k_segment.reshape(1, window), k_index.reshape(1, window))


def local(hidden_in, norm_gain, query_proj, kv_proj, prompt_lengths, cache_slot):
    count_gx = lax.axis_size(GX)
    count_gy = lax.axis_size(GY)
    where_gx = lax.axis_index(GX)
    where_gy = lax.axis_index(GY)
    local_rows, local_feats = hidden_in.shape
    features = local_feats * count_gy
    block_tokens = local_rows * count_gx // count_gy
    all_tokens = block_tokens * count_gy
    blocks_per_slab = local_rows // block_tokens
    sub = block_tokens // count_gy
    heads_here = query_proj.shape[0] // HD
    query_cols = heads_here * HD
    is_key = where_gx % 2 == 0

    kv_rows = lax.dynamic_slice_in_dim(kv_proj, where_gx * HD, HD, 0)
    gain_rows = jnp.concatenate(
        [norm_gain[None, :], jnp.zeros((7, local_feats), norm_gain.dtype)], axis=0
    )
    stacked = jnp.concatenate([query_proj, kv_rows, gain_rows], axis=0)
    gathered = lax.all_gather(stacked, "z", axis=1, tiled=True)
    gathered = lax.all_gather(gathered, "y", axis=1, tiled=True)
    weight_rows = query_cols + HD
    weights_full = gathered[:weight_rows]
    gain_full = gathered[weight_rows]

    pieces = hidden_in.reshape(blocks_per_slab, count_gy, sub, local_feats)
    pieces = lax.all_to_all(pieces, GY, 1, 1, tiled=True)
    spread = jnp.broadcast_to(pieces[None], (count_gx,) + pieces.shape)
    rows_here = lax.all_to_all(spread, GX, 0, 0, tiled=True)
    rows_here = rows_here.transpose(0, 1, 3, 2, 4).reshape(block_tokens, features)
    widened = rows_here.astype(jnp.float32)
    squares = jnp.sum(widened * widened, axis=1)
    normed = (
        widened * lax.rsqrt(squares / features + epsilon)[:, None]
        * gain_full.astype(jnp.float32)[None, :]
    ).astype(jnp.bfloat16)
    contract = (((1,), (1,)), ((), ()))
    projected = lax.dot_general(normed, weights_full, contract, preferred_element_type=jnp.float32)

    order = jnp.arange(block_tokens, dtype=jnp.int32)
    my_tokens = (order // sub) * block_tokens + where_gy * sub + order % sub
    unused_segment, my_places = token_places(prompt_lengths, my_tokens)
    queries = rotate(
        projected[:, :query_cols].reshape(block_tokens, heads_here, HD), my_places
    ).astype(jnp.bfloat16)
    half_raw = projected[:, query_cols:]
    rotated = rotate(half_raw[:, None, :], my_places)[:, 0, :]
    mine = jnp.where(is_key, rotated, half_raw).astype(jnp.bfloat16)

    needed_blocks = MOST // block_tokens + 1
    window_blocks = min(count_gy, -(-needed_blocks * sub // 16) * 16 // sub)
    window = window_blocks * block_tokens
    first_blocks = [min(max(b - (window_blocks - 1), 0), count_gy - window_blocks) for b in range(count_gy)]
    chosen = jnp.asarray(
        [[f + w for w in range(window_blocks)] for f in first_blocks], dtype=jnp.int32
    )
    strided = mine.reshape(count_gy, sub, HD)
    kv_parcel = jnp.take(strided, chosen, axis=0).reshape(count_gy, window_blocks * sub, HD)
    q_parcel = queries.reshape(count_gy, sub * heads_here, HD)
    parcel = jnp.concatenate([q_parcel, kv_parcel], axis=1)
    arrived = lax.all_to_all(parcel, GY, 0, 0, tiled=True)
    queries = arrived[:, : sub * heads_here].reshape(block_tokens, query_cols)
    mine_window = arrived[:, sub * heads_here :]
    other_window = lax.ppermute(mine_window, GX, [(p, p ^ 1) for p in range(count_gx)])
    key_rows = jnp.where(is_key, mine_window, other_window).reshape(window, HD)
    value_rows = jnp.where(is_key, other_window, mine_window).reshape(window, HD)

    first_query = where_gy * block_tokens
    token_index = first_query + order
    segment_own, unused_places = token_places(prompt_lengths, token_index)
    window_first = jnp.clip(where_gy - (window_blocks - 1), 0, count_gy - window_blocks)
    source_range = jnp.arange(count_gy, dtype=jnp.int32)[:, None, None]
    block_range = jnp.arange(window_blocks, dtype=jnp.int32)[None, :, None]
    sub_range = jnp.arange(sub, dtype=jnp.int32)[None, None, :]
    key_index = (
        (window_first + block_range) * block_tokens + source_range * sub + sub_range
    ).reshape(window)
    key_segment, unused_places = token_places(prompt_lengths, key_index)
    attention = segment_attention(
        queries, key_rows, value_rows,
        segment_own, token_index, key_segment, key_index, HD,
    )

    cache_cols = lax.dynamic_index_in_dim(
        mine_window.reshape(count_gy, window_blocks, sub, HD), where_gy - window_first, 1, keepdims=False
    ).reshape(block_tokens, HD)
    pages_dev = PAGES_DEV
    page_len = block_tokens // pages_dev
    page_range = jnp.arange(pages_dev, dtype=jnp.int32)
    width_cols = cache_cols.shape[1]
    my_pages = cache_cols.reshape(pages_dev, page_len * width_cols)
    capacity = max(1, pages_dev // count_gy)
    slots_all = count_gy * capacity
    owners = (cache_slot // pages_dev).reshape(count_gy, pages_dev)
    earlier = page_range[None, :] < page_range[:, None]
    same_owner = owners[:, :, None] == owners[:, None, :]
    ranks = jnp.sum((same_owner & earlier[None]).astype(jnp.int32), axis=2)
    my_owner = lax.dynamic_index_in_dim(owners, where_gy, 0, keepdims=False)
    my_rank = lax.dynamic_index_in_dim(ranks, where_gy, 0, keepdims=False)
    target = my_owner * capacity + my_rank
    slot_range = jnp.arange(slots_all, dtype=jnp.int32)
    send_map = (slot_range[:, None] == target[None, :]).astype(jnp.bfloat16)
    outgoing = jnp.dot(send_map, my_pages, preferred_element_type=jnp.float32).astype(jnp.bfloat16)
    incoming = lax.all_to_all(outgoing, GY, split_axis=0, concat_axis=0, tiled=True)
    wanted = where_gy * pages_dev + page_range
    matches = cache_slot[None, :] == wanted[:, None]
    page_ids = jnp.arange(cache_slot.shape[0], dtype=jnp.int32)
    source_page = jnp.sum(jnp.where(matches, page_ids[None, :], 0), axis=1)
    source_rank = jnp.sum(jnp.where(matches, ranks.reshape(-1)[None, :], 0), axis=1)
    source_slot = source_page // pages_dev * capacity + source_rank
    take_map = (source_slot[:, None] == slot_range[None, :]).astype(jnp.bfloat16)
    cache_block = jnp.dot(take_map, incoming, preferred_element_type=jnp.float32)
    cache_block = cache_block.astype(jnp.bfloat16).reshape(pages_dev, page_len, width_cols)
    return (attention, cache_block)


def solution(mesh):
    parts = mesh.devices.reshape(4, 2, 4, 8)
    split_mesh = jax.sharding.Mesh(parts, ("x", "core", "y", "z"))
    return jax.shard_map(
        local,
        mesh=split_mesh,
        in_specs=(P(GX, GY), P(GY), P(GX, GY), P(None, GY), P(), P()),
        out_specs=(P(GY, GX), P(GY, None, GX)),
        check_vma=False,
    )
```

```python
import functools
import math

import jax
import jax.numpy as jnp
from jax import lax
from jax.experimental import pallas as pl
from jax.experimental.pallas import tpu as pltpu
from jax.sharding import PartitionSpec as P

D = 4096
H = 32
KVH = 4
HD = 128
PAGES_DEV = 16
MOST = 4096


epsilon = 1e-06
rope_base = 5000000.0
masked_out = -1e30


def token_places(prompt_lengths, token_index):
    prompt_ends = jnp.cumsum(prompt_lengths)
    prompt_starts = prompt_ends - prompt_lengths
    segment = jnp.sum((token_index[:, None] >= prompt_ends[None, :]).astype(jnp.int32), axis=1)
    chosen = segment[:, None] == jnp.arange(prompt_lengths.shape[0], dtype=jnp.int32)[None, :]
    opening = jnp.sum(jnp.where(chosen, prompt_starts[None, :], 0), axis=1)
    return (segment, token_index - opening)


def rotate(vectors, places):
    half_size = vectors.shape[-1] // 2
    frequency = rope_base ** (-(jnp.arange(half_size, dtype=jnp.float32) * 2.0) / vectors.shape[-1])
    angles = places.astype(jnp.float32)[:, None] * frequency[None, :]
    cos_part = jnp.cos(angles)[:, None, :]
    sin_part = jnp.sin(angles)[:, None, :]
    leading = vectors[..., :half_size]
    trailing = vectors[..., half_size:]
    return jnp.concatenate(
        [leading * cos_part - trailing * sin_part, trailing * cos_part + leading * sin_part],
        axis=-1,
    )


def attention_heads(scale, heads, head_size, q_ref, k_ref, v_ref, allowed, o_ref):
    for h in range(heads):
        columns = slice(h * head_size, (h + 1) * head_size)
        scores = lax.dot_general(
            q_ref[:, columns], k_ref[...], (((1,), (1,)), ((), ())),
            preferred_element_type=jnp.float32,
        ) * scale
        scores = jnp.where(allowed, scores, masked_out)
        row_max = jnp.max(scores, axis=1, keepdims=True)
        weights = jnp.exp(scores - row_max)
        totals = jnp.sum(weights, axis=1, keepdims=True)
        mixed = jnp.dot(weights.astype(jnp.bfloat16), v_ref[...], preferred_element_type=jnp.float32)
        o_ref[:, columns] = (mixed / totals).astype(o_ref.dtype)


def attention_body(scale, heads, head_size, flag_ref, q_ref, a_ref, b_ref, qseg_ref, qidx_ref, kseg_ref, kidx_ref, o_ref):
    allowed = (kseg_ref[...] == qseg_ref[...]) & (kidx_ref[...] <= qidx_ref[...])

    @pl.when(flag_ref[0] == 1)
    def _():
        attention_heads(scale, heads, head_size, q_ref, a_ref, b_ref, allowed, o_ref)

    @pl.when(flag_ref[0] != 1)
    def _():
        attention_heads(scale, heads, head_size, q_ref, b_ref, a_ref, allowed, o_ref)


def segment_attention(a_is_key, queries, a_rows, b_rows, q_segment, q_index, k_segment, k_index, head_size, row_chunk=128):
    tokens, cols = queries.shape
    heads = cols // head_size
    window = a_rows.shape[0]
    flops = 4 * tokens * window * head_size * heads
    grid_spec = pltpu.PrefetchScalarGridSpec(
        num_scalar_prefetch=1,
        grid=(tokens // row_chunk,),
        in_specs=[
            pl.BlockSpec((row_chunk, cols), lambda r, f: (r, 0)),
            pl.BlockSpec((window, head_size), lambda r, f: (0, 0)),
            pl.BlockSpec((window, head_size), lambda r, f: (0, 0)),
            pl.BlockSpec((row_chunk, 1), lambda r, f: (r, 0)),
            pl.BlockSpec((row_chunk, 1), lambda r, f: (r, 0)),
            pl.BlockSpec((1, window), lambda r, f: (0, 0)),
            pl.BlockSpec((1, window), lambda r, f: (0, 0)),
        ],
        out_specs=pl.BlockSpec((row_chunk, cols), lambda r, f: (r, 0)),
    )
    return pl.pallas_call(
        functools.partial(attention_body, 1.0 / math.sqrt(head_size), heads, head_size),
        grid_spec=grid_spec,
        out_shape=jax.ShapeDtypeStruct((tokens, cols), jnp.bfloat16),
        cost_estimate=pl.CostEstimate(
            flops=flops, transcendentals=tokens * window * heads,
            bytes_accessed=2 * (2 * tokens * cols + 2 * window * head_size) + 8 * (tokens + window),
        ),
    )(a_is_key.astype(jnp.int32).reshape(1), queries, a_rows, b_rows,
      q_segment.reshape(tokens, 1), q_index.reshape(tokens, 1),
      k_segment.reshape(1, window), k_index.reshape(1, window))


def local(hidden_in, norm_gain, query_proj, kv_proj, prompt_lengths, cache_slot):
    count_gx = lax.axis_size("gx")
    count_gy = lax.axis_size("gy")
    where_gx = lax.axis_index("gx")
    where_gy = lax.axis_index("gy")
    local_rows, local_feats = hidden_in.shape
    features = local_feats * count_gy
    block_tokens = local_rows * count_gx // count_gy
    all_tokens = block_tokens * count_gy
    blocks_per_slab = local_rows // block_tokens
    sub = block_tokens // count_gy
    heads_here = query_proj.shape[0] // HD
    query_cols = heads_here * HD
    is_key = where_gx % 2 == 0

    kv_rows = lax.dynamic_slice_in_dim(kv_proj, where_gx * HD, HD, 0)
    gain_rows = jnp.concatenate(
        [norm_gain[None, :], jnp.zeros((7, local_feats), norm_gain.dtype)], axis=0
    )
    stacked = jnp.concatenate([query_proj, kv_rows, gain_rows], axis=0)
    gathered = lax.all_gather(stacked, "gy", axis=1, tiled=True)
    weight_rows = query_cols + HD
    weights_full = gathered[:weight_rows]
    gain_full = gathered[weight_rows]

    pieces = hidden_in.reshape(blocks_per_slab, count_gy, sub, local_feats)
    pieces = lax.all_to_all(pieces, "gy", 1, 1, tiled=True)
    spread = jnp.broadcast_to(pieces[None], (count_gx,) + pieces.shape)
    rows_here = lax.all_to_all(spread, "gx", 0, 0, tiled=True)
    rows_here = rows_here.transpose(0, 1, 3, 2, 4).reshape(block_tokens, features)
    widened = rows_here.astype(jnp.float32)
    squares = jnp.sum(widened * widened, axis=1)
    normed = (
        widened * lax.rsqrt(squares / features + epsilon)[:, None]
        * gain_full.astype(jnp.float32)[None, :]
    ).astype(jnp.bfloat16)
    contract = (((1,), (1,)), ((), ()))
    projected = lax.dot_general(normed, weights_full, contract, preferred_element_type=jnp.float32)

    order = jnp.arange(block_tokens, dtype=jnp.int32)
    my_tokens = (order // sub) * block_tokens + where_gy * sub + order % sub
    unused_segment, my_places = token_places(prompt_lengths, my_tokens)
    queries = rotate(
        projected[:, :query_cols].reshape(block_tokens, heads_here, HD), my_places
    ).astype(jnp.bfloat16)
    half_raw = projected[:, query_cols:]
    rotated = rotate(half_raw[:, None, :], my_places)[:, 0, :]
    mine = jnp.where(is_key, rotated, half_raw).astype(jnp.bfloat16)

    needed_blocks = MOST // block_tokens + 1
    window_blocks = min(count_gy, -(-needed_blocks * sub // 16) * 16 // sub)
    window = window_blocks * block_tokens
    first_blocks = [min(max(b - (window_blocks - 1), 0), count_gy - window_blocks) for b in range(count_gy)]
    chosen = jnp.asarray(
        [[f + w for w in range(window_blocks)] for f in first_blocks], dtype=jnp.int32
    )
    strided = mine.reshape(count_gy, sub, HD)
    kv_parcel = jnp.take(strided, chosen, axis=0).reshape(count_gy, window_blocks * sub, HD)
    q_parcel = queries.reshape(count_gy, sub * heads_here, HD)
    parcel = jnp.concatenate([q_parcel, kv_parcel], axis=1)
    arrived = lax.all_to_all(parcel, "gy", 0, 0, tiled=True)
    queries = arrived[:, : sub * heads_here].reshape(block_tokens, query_cols)
    mine_window = arrived[:, sub * heads_here :]
    other_window = lax.ppermute(mine_window, "gx", [(p, p ^ 1) for p in range(count_gx)])

    first_query = where_gy * block_tokens
    token_index = first_query + order
    segment_own, unused_places = token_places(prompt_lengths, token_index)
    window_first = jnp.clip(where_gy - (window_blocks - 1), 0, count_gy - window_blocks)
    source_range = jnp.arange(count_gy, dtype=jnp.int32)[:, None, None]
    block_range = jnp.arange(window_blocks, dtype=jnp.int32)[None, :, None]
    sub_range = jnp.arange(sub, dtype=jnp.int32)[None, None, :]
    key_index = (
        (window_first + block_range) * block_tokens + source_range * sub + sub_range
    ).reshape(window)
    key_segment, unused_places = token_places(prompt_lengths, key_index)
    attention = segment_attention(
        is_key, queries, mine_window.reshape(window, HD), other_window.reshape(window, HD),
        segment_own, token_index, key_segment, key_index, HD,
    )

    cache_cols = lax.dynamic_index_in_dim(
        mine_window.reshape(count_gy, window_blocks, sub, HD), where_gy - window_first, 1, keepdims=False
    ).reshape(block_tokens, HD)
    pages_dev = PAGES_DEV
    page_len = block_tokens // pages_dev
    page_range = jnp.arange(pages_dev, dtype=jnp.int32)
    width_cols = cache_cols.shape[1]
    my_pages = cache_cols.reshape(pages_dev, page_len * width_cols)
    capacity = max(1, pages_dev // count_gy)
    slots_all = count_gy * capacity
    owners = (cache_slot // pages_dev).reshape(count_gy, pages_dev)
    earlier = page_range[None, :] < page_range[:, None]
    same_owner = owners[:, :, None] == owners[:, None, :]
    ranks = jnp.sum((same_owner & earlier[None]).astype(jnp.int32), axis=2)
    my_owner = lax.dynamic_index_in_dim(owners, where_gy, 0, keepdims=False)
    my_rank = lax.dynamic_index_in_dim(ranks, where_gy, 0, keepdims=False)
    target = my_owner * capacity + my_rank
    slot_range = jnp.arange(slots_all, dtype=jnp.int32)
    send_map = (slot_range[:, None] == target[None, :]).astype(jnp.bfloat16)
    outgoing = jnp.dot(send_map, my_pages, preferred_element_type=jnp.float32).astype(jnp.bfloat16)
    incoming = lax.all_to_all(outgoing, "gy", split_axis=0, concat_axis=0, tiled=True)
    wanted = where_gy * pages_dev + page_range
    matches = cache_slot[None, :] == wanted[:, None]
    page_ids = jnp.arange(cache_slot.shape[0], dtype=jnp.int32)
    source_page = jnp.sum(jnp.where(matches, page_ids[None, :], 0), axis=1)
    source_rank = jnp.sum(jnp.where(matches, ranks.reshape(-1)[None, :], 0), axis=1)
    source_slot = source_page // pages_dev * capacity + source_rank
    take_map = (source_slot[:, None] == slot_range[None, :]).astype(jnp.bfloat16)
    cache_block = jnp.dot(take_map, incoming, preferred_element_type=jnp.float32)
    cache_block = cache_block.astype(jnp.bfloat16).reshape(pages_dev, page_len, width_cols)
    return (attention, cache_block)


def solution(mesh):
    return jax.shard_map(
        local,
        mesh=mesh,
        in_specs=(P("gx", "gy"), P("gy"), P("gx", "gy"), P(None, "gy"), P(), P()),
        out_specs=(P("gy", "gx"), P("gy", None, "gx")),
        check_vma=False,
    )
```

```python
import functools
import math

import jax
import jax.numpy as jnp
from jax import lax
from jax.experimental import pallas as pl
from jax.experimental.pallas import tpu as pltpu
from jax.sharding import PartitionSpec as P


HD = 128
PAGES_DEV = 16
MOST = 4096


epsilon = 1e-06
rope_base = 5000000.0
masked_out = -1e30


def token_places(prompt_lengths, token_index):
    prompt_ends = jnp.cumsum(prompt_lengths)
    prompt_starts = prompt_ends - prompt_lengths
    segment = jnp.sum((token_index[:, None] >= prompt_ends[None, :]).astype(jnp.int32), axis=1)
    chosen = segment[:, None] == jnp.arange(prompt_lengths.shape[0], dtype=jnp.int32)[None, :]
    opening = jnp.sum(jnp.where(chosen, prompt_starts[None, :], 0), axis=1)
    return (segment, token_index - opening)


def rotate(vectors, places):
    half_size = vectors.shape[-1] // 2
    frequency = rope_base ** (-(jnp.arange(half_size, dtype=jnp.float32) * 2.0) / vectors.shape[-1])
    angles = places.astype(jnp.float32)[:, None] * frequency[None, :]
    cos_part = jnp.cos(angles)[:, None, :]
    sin_part = jnp.sin(angles)[:, None, :]
    leading = vectors[..., :half_size]
    trailing = vectors[..., half_size:]
    return jnp.concatenate(
        [leading * cos_part - trailing * sin_part, trailing * cos_part + leading * sin_part],
        axis=-1,
    )


def attention_heads(scale, heads, head_size, q_ref, k_ref, v_ref, allowed, o_ref):
    for h in range(heads):
        columns = slice(h * head_size, (h + 1) * head_size)
        scores = lax.dot_general(
            q_ref[:, columns], k_ref[...], (((1,), (1,)), ((), ())),
            preferred_element_type=jnp.float32,
        ) * scale
        scores = jnp.where(allowed, scores, masked_out)
        row_max = jnp.max(scores, axis=1, keepdims=True)
        weights = jnp.exp(scores - row_max)
        totals = jnp.sum(weights, axis=1, keepdims=True)
        mixed = jnp.dot(weights.astype(jnp.bfloat16), v_ref[...], preferred_element_type=jnp.float32)
        o_ref[:, columns] = (mixed / totals).astype(o_ref.dtype)


def attention_body(scale, heads, head_size, flag_ref, q_ref, a_ref, b_ref, qseg_ref, qidx_ref, kseg_ref, kidx_ref, o_ref):
    allowed = (kseg_ref[...] == qseg_ref[...]) & (kidx_ref[...] <= qidx_ref[...])

    @pl.when(flag_ref[0] == 1)
    def _():
        attention_heads(scale, heads, head_size, q_ref, a_ref, b_ref, allowed, o_ref)

    @pl.when(flag_ref[0] != 1)
    def _():
        attention_heads(scale, heads, head_size, q_ref, b_ref, a_ref, allowed, o_ref)


def segment_attention(a_is_key, queries, a_rows, b_rows, q_segment, q_index, k_segment, k_index, head_size, row_chunk=128):
    tokens, cols = queries.shape
    heads = cols // head_size
    window = a_rows.shape[0]
    flops = 4 * tokens * window * head_size * heads
    grid_spec = pltpu.PrefetchScalarGridSpec(
        num_scalar_prefetch=1,
        grid=(tokens // row_chunk,),
        in_specs=[
            pl.BlockSpec((row_chunk, cols), lambda r, f: (r, 0)),
            pl.BlockSpec((window, head_size), lambda r, f: (0, 0)),
            pl.BlockSpec((window, head_size), lambda r, f: (0, 0)),
            pl.BlockSpec((row_chunk, 1), lambda r, f: (r, 0)),
            pl.BlockSpec((row_chunk, 1), lambda r, f: (r, 0)),
            pl.BlockSpec((1, window), lambda r, f: (0, 0)),
            pl.BlockSpec((1, window), lambda r, f: (0, 0)),
        ],
        out_specs=pl.BlockSpec((row_chunk, cols), lambda r, f: (r, 0)),
    )
    return pl.pallas_call(
        functools.partial(attention_body, 1.0 / math.sqrt(head_size), heads, head_size),
        grid_spec=grid_spec,
        out_shape=jax.ShapeDtypeStruct((tokens, cols), jnp.bfloat16),
        cost_estimate=pl.CostEstimate(
            flops=flops, transcendentals=tokens * window * heads,
            bytes_accessed=2 * (2 * tokens * cols + 2 * window * head_size) + 8 * (tokens + window),
        ),
    )(a_is_key.astype(jnp.int32).reshape(1), queries, a_rows, b_rows,
      q_segment.reshape(tokens, 1), q_index.reshape(tokens, 1),
      k_segment.reshape(1, window), k_index.reshape(1, window))


def local(hidden_in, norm_gain, query_proj, kv_proj, prompt_lengths, cache_slot):
    count_gx = lax.axis_size("gx")
    count_gy = lax.axis_size("gy")
    where_gx = lax.axis_index("gx")
    where_gy = lax.axis_index("gy")
    local_rows, local_feats = hidden_in.shape
    features = local_feats * count_gy
    block_tokens = local_rows * count_gx // count_gy
    blocks_per_slab = local_rows // block_tokens
    sub = block_tokens // count_gy
    heads_here = query_proj.shape[0] // HD
    query_cols = heads_here * HD
    is_key = where_gx % 2 == 0

    kv_rows = lax.dynamic_slice_in_dim(kv_proj, where_gx * HD, HD, 0)
    gain_rows = jnp.concatenate(
        [norm_gain[None, :], jnp.zeros((7, local_feats), norm_gain.dtype)], axis=0
    )
    stacked = jnp.concatenate([query_proj, kv_rows, gain_rows], axis=0)
    gathered = lax.all_gather(stacked, "gy", axis=1, tiled=True)
    weight_rows = query_cols + HD
    weights_full = gathered[:weight_rows]
    gain_full = gathered[weight_rows]

    pieces = hidden_in.reshape(blocks_per_slab, count_gy, sub, local_feats)
    pieces = lax.all_to_all(pieces, "gy", 1, 1, tiled=True)
    spread = jnp.broadcast_to(pieces[None], (count_gx,) + pieces.shape)
    rows_here = lax.all_to_all(spread, "gx", 0, 0, tiled=True)
    rows_here = rows_here.transpose(0, 1, 3, 2, 4).reshape(block_tokens, features)
    widened = rows_here.astype(jnp.float32)
    squares = jnp.sum(widened * widened, axis=1)
    normed = (
        widened * lax.rsqrt(squares / features + epsilon)[:, None]
        * gain_full.astype(jnp.float32)[None, :]
    ).astype(jnp.bfloat16)
    contract = (((1,), (1,)), ((), ()))
    projected = lax.dot_general(normed, weights_full, contract, preferred_element_type=jnp.float32)

    order = jnp.arange(block_tokens, dtype=jnp.int32)
    my_tokens = (order // sub) * block_tokens + where_gy * sub + order % sub
    _, my_places = token_places(prompt_lengths, my_tokens)
    queries = rotate(
        projected[:, :query_cols].reshape(block_tokens, heads_here, HD), my_places
    ).astype(jnp.bfloat16)
    half_raw = projected[:, query_cols:]
    rotated = rotate(half_raw[:, None, :], my_places)[:, 0, :]
    mine = jnp.where(is_key, rotated, half_raw).astype(jnp.bfloat16)

    needed_blocks = MOST // block_tokens + 1
    window_blocks = min(count_gy, -(-needed_blocks * sub // 16) * 16 // sub)
    window = window_blocks * block_tokens
    first_blocks = [min(max(b - (window_blocks - 1), 0), count_gy - window_blocks) for b in range(count_gy)]
    chosen = jnp.asarray(
        [[f + w for w in range(window_blocks)] for f in first_blocks], dtype=jnp.int32
    )
    strided = mine.reshape(count_gy, sub, HD)
    kv_parcel = jnp.take(strided, chosen, axis=0).reshape(count_gy, window_blocks * sub, HD)
    q_parcel = queries.reshape(count_gy, sub * heads_here, HD)
    parcel = jnp.concatenate([q_parcel, kv_parcel], axis=1)
    arrived = lax.all_to_all(parcel, "gy", 0, 0, tiled=True)
    queries = arrived[:, : sub * heads_here].reshape(block_tokens, query_cols)
    mine_window = arrived[:, sub * heads_here :]
    other_window = lax.ppermute(mine_window, "gx", [(p, p ^ 1) for p in range(count_gx)])

    first_query = where_gy * block_tokens
    token_index = first_query + order
    segment_own, unused_places = token_places(prompt_lengths, token_index)
    window_first = jnp.clip(where_gy - (window_blocks - 1), 0, count_gy - window_blocks)
    source_range = jnp.arange(count_gy, dtype=jnp.int32)[:, None, None]
    block_range = jnp.arange(window_blocks, dtype=jnp.int32)[None, :, None]
    sub_range = jnp.arange(sub, dtype=jnp.int32)[None, None, :]
    key_index = (
        (window_first + block_range) * block_tokens + source_range * sub + sub_range
    ).reshape(window)
    key_segment, unused_places = token_places(prompt_lengths, key_index)
    attention = segment_attention(
        is_key, queries, mine_window.reshape(window, HD), other_window.reshape(window, HD),
        segment_own, token_index, key_segment, key_index, HD,
    )

    cache_cols = lax.dynamic_index_in_dim(
        mine_window.reshape(count_gy, window_blocks, sub, HD), where_gy - window_first, 1, keepdims=False
    ).reshape(block_tokens, HD)
    pages_dev = PAGES_DEV
    page_len = block_tokens // pages_dev
    page_range = jnp.arange(pages_dev, dtype=jnp.int32)
    width_cols = cache_cols.shape[1]
    my_pages = cache_cols.reshape(pages_dev, page_len * width_cols)
    capacity = max(1, pages_dev // count_gy)
    slots_all = count_gy * capacity
    owners = (cache_slot // pages_dev).reshape(count_gy, pages_dev)
    earlier = page_range[None, :] < page_range[:, None]
    same_owner = owners[:, :, None] == owners[:, None, :]
    ranks = jnp.sum((same_owner & earlier[None]).astype(jnp.int32), axis=2)
    my_owner = lax.dynamic_index_in_dim(owners, where_gy, 0, keepdims=False)
    my_rank = lax.dynamic_index_in_dim(ranks, where_gy, 0, keepdims=False)
    target = my_owner * capacity + my_rank
    slot_range = jnp.arange(slots_all, dtype=jnp.int32)
    send_map = (slot_range[:, None] == target[None, :]).astype(jnp.bfloat16)
    outgoing = jnp.dot(send_map, my_pages, preferred_element_type=jnp.float32).astype(jnp.bfloat16)
    incoming = lax.all_to_all(outgoing, "gy", split_axis=0, concat_axis=0, tiled=True)
    wanted = where_gy * pages_dev + page_range
    matches = cache_slot[None, :] == wanted[:, None]
    page_ids = jnp.arange(cache_slot.shape[0], dtype=jnp.int32)
    source_page = jnp.sum(jnp.where(matches, page_ids[None, :], 0), axis=1)
    source_rank = jnp.sum(jnp.where(matches, ranks.reshape(-1)[None, :], 0), axis=1)
    source_slot = source_page // pages_dev * capacity + source_rank
    take_map = (source_slot[:, None] == slot_range[None, :]).astype(jnp.bfloat16)
    cache_block = jnp.dot(take_map, incoming, preferred_element_type=jnp.float32)
    cache_block = cache_block.astype(jnp.bfloat16).reshape(pages_dev, page_len, width_cols)
    return (attention, cache_block)


def solution(mesh):
    return jax.shard_map(
        local,
        mesh=mesh,
        in_specs=(P("gx", "gy"), P("gy"), P("gx", "gy"), P(None, "gy"), P(), P()),
        out_specs=(P("gy", "gx"), P("gy", None, "gx")),
        check_vma=False,
    )
```

```python
import functools
import math

import jax
import jax.numpy as jnp
from jax import lax
from jax.experimental import pallas as pl
from jax.experimental.pallas import tpu as pltpu
from jax.sharding import PartitionSpec as P


HD = 128
PAGES_DEV = 16
MOST = 4096


epsilon = 1e-06
rope_base = 5000000.0
masked_out = -1e30


def token_places(prompt_lengths, token_index):
    prompt_ends = jnp.cumsum(prompt_lengths)
    prompt_starts = prompt_ends - prompt_lengths
    segment = jnp.sum((token_index[:, None] >= prompt_ends[None, :]).astype(jnp.int32), axis=1)
    chosen = segment[:, None] == jnp.arange(prompt_lengths.shape[0], dtype=jnp.int32)[None, :]
    opening = jnp.sum(jnp.where(chosen, prompt_starts[None, :], 0), axis=1)
    return (segment, token_index - opening)


def rotate(vectors, places):
    half_size = vectors.shape[-1] // 2
    frequency = rope_base ** (-(jnp.arange(half_size, dtype=jnp.float32) * 2.0) / vectors.shape[-1])
    angles = places.astype(jnp.float32)[:, None] * frequency[None, :]
    cos_part = jnp.cos(angles)[:, None, :]
    sin_part = jnp.sin(angles)[:, None, :]
    leading = vectors[..., :half_size]
    trailing = vectors[..., half_size:]
    return jnp.concatenate(
        [leading * cos_part - trailing * sin_part, trailing * cos_part + leading * sin_part],
        axis=-1,
    )


def attention_heads(scale, heads, head_size, q_ref, k_ref, v_ref, allowed, o_ref):
    for h in range(heads):
        columns = slice(h * head_size, (h + 1) * head_size)
        scores = lax.dot_general(
            q_ref[:, columns], k_ref[...], (((1,), (1,)), ((), ())),
            preferred_element_type=jnp.float32,
        ) * scale
        scores = jnp.where(allowed, scores, masked_out)
        row_max = jnp.max(scores, axis=1, keepdims=True)
        weights = jnp.exp(scores - row_max)
        totals = jnp.sum(weights, axis=1, keepdims=True)
        mixed = jnp.dot(weights.astype(jnp.bfloat16), v_ref[...], preferred_element_type=jnp.float32)
        o_ref[:, columns] = (mixed / totals).astype(o_ref.dtype)


def attention_body(scale, heads, head_size, flag_ref, q_ref, a_ref, b_ref, qseg_ref, qidx_ref, kseg_ref, kidx_ref, o_ref):
    allowed = (kseg_ref[...] == qseg_ref[...]) & (kidx_ref[...] <= qidx_ref[...])

    @pl.when(flag_ref[0] == 1)
    def _():
        attention_heads(scale, heads, head_size, q_ref, a_ref, b_ref, allowed, o_ref)

    @pl.when(flag_ref[0] != 1)
    def _():
        attention_heads(scale, heads, head_size, q_ref, b_ref, a_ref, allowed, o_ref)


def segment_attention(a_is_key, queries, a_rows, b_rows, q_segment, q_index, k_segment, k_index, head_size, row_chunk=256):
    tokens, cols = queries.shape
    heads = cols // head_size
    window = a_rows.shape[0]
    flops = 4 * tokens * window * head_size * heads
    grid_spec = pltpu.PrefetchScalarGridSpec(
        num_scalar_prefetch=1,
        grid=(tokens // row_chunk,),
        in_specs=[
            pl.BlockSpec((row_chunk, cols), lambda r, f: (r, 0)),
            pl.BlockSpec((window, head_size), lambda r, f: (0, 0)),
            pl.BlockSpec((window, head_size), lambda r, f: (0, 0)),
            pl.BlockSpec((row_chunk, 1), lambda r, f: (r, 0)),
            pl.BlockSpec((row_chunk, 1), lambda r, f: (r, 0)),
            pl.BlockSpec((1, window), lambda r, f: (0, 0)),
            pl.BlockSpec((1, window), lambda r, f: (0, 0)),
        ],
        out_specs=pl.BlockSpec((row_chunk, cols), lambda r, f: (r, 0)),
    )
    return pl.pallas_call(
        functools.partial(attention_body, 1.0 / math.sqrt(head_size), heads, head_size),
        grid_spec=grid_spec,
        out_shape=jax.ShapeDtypeStruct((tokens, cols), jnp.bfloat16),
        cost_estimate=pl.CostEstimate(
            flops=flops, transcendentals=tokens * window * heads,
            bytes_accessed=2 * (2 * tokens * cols + 2 * window * head_size) + 8 * (tokens + window),
        ),
    )(a_is_key.astype(jnp.int32).reshape(1), queries, a_rows, b_rows, q_segment, q_index, k_segment, k_index)


def local(hidden_in, norm_gain, query_proj, kv_proj, prompt_lengths, cache_slot):
    count_gx = lax.axis_size("gx")
    count_gy = lax.axis_size("gy")
    where_gx = lax.axis_index("gx")
    where_gy = lax.axis_index("gy")
    local_rows, local_feats = hidden_in.shape
    features = local_feats * count_gy
    block_tokens = local_rows * count_gx // count_gy
    blocks_per_slab = local_rows // block_tokens
    sub = block_tokens // count_gy
    heads_here = query_proj.shape[0] // HD
    query_cols = heads_here * HD
    is_key = where_gx % 2 == 0

    kv_rows = lax.dynamic_slice_in_dim(kv_proj, where_gx * HD, HD, 0)
    gain_rows = jnp.concatenate(
        [norm_gain[None, :], jnp.zeros((7, local_feats), norm_gain.dtype)], axis=0
    )
    stacked = jnp.concatenate([query_proj, kv_rows, gain_rows], axis=0)
    gathered = lax.all_gather(stacked, "gy", axis=1, tiled=True)
    weight_rows = query_cols + HD
    weights_full = gathered[:weight_rows]
    gain_full = gathered[weight_rows]

    pieces = hidden_in.reshape(blocks_per_slab, count_gy, sub, local_feats)
    pieces = lax.all_to_all(pieces, "gy", 1, 1, tiled=True)
    spread = jnp.broadcast_to(pieces[None], (count_gx,) + pieces.shape)
    rows_here = lax.all_to_all(spread, "gx", 0, 0, tiled=True)
    rows_here = rows_here.transpose(0, 1, 3, 2, 4).reshape(block_tokens, features)
    needed_blocks = MOST // block_tokens + 1
    window_blocks = min(count_gy, -(-needed_blocks * sub // 16) * 16 // sub)
    window = window_blocks * block_tokens
    order = jnp.arange(block_tokens, dtype=jnp.int32)
    first_query = where_gy * block_tokens
    token_index = first_query + order
    segment_own, unused_places = token_places(prompt_lengths, token_index)
    window_first = jnp.clip(where_gy - (window_blocks - 1), 0, count_gy - window_blocks)
    source_range = jnp.arange(count_gy, dtype=jnp.int32)[:, None, None]
    block_range = jnp.arange(window_blocks, dtype=jnp.int32)[None, :, None]
    sub_range = jnp.arange(sub, dtype=jnp.int32)[None, None, :]
    key_index = (
        (window_first + block_range) * block_tokens + source_range * sub + sub_range
    ).reshape(window)
    key_segment, unused_places = token_places(prompt_lengths, key_index)
    q_segment = segment_own.reshape(block_tokens, 1)
    q_index = token_index.reshape(block_tokens, 1)
    k_segment = key_segment.reshape(1, window)
    k_index = key_index.reshape(1, window)
    rows_here, q_segment, q_index, k_segment, k_index = lax.optimization_barrier(
        (rows_here, q_segment, q_index, k_segment, k_index)
    )
    widened = rows_here.astype(jnp.float32)
    squares = jnp.sum(widened * widened, axis=1)
    normed = (
        widened * lax.rsqrt(squares / features + epsilon)[:, None]
        * gain_full.astype(jnp.float32)[None, :]
    ).astype(jnp.bfloat16)
    contract = (((1,), (1,)), ((), ()))
    projected = lax.dot_general(normed, weights_full, contract, preferred_element_type=jnp.float32)

    my_tokens = (order // sub) * block_tokens + where_gy * sub + order % sub
    _, my_places = token_places(prompt_lengths, my_tokens)
    queries = rotate(
        projected[:, :query_cols].reshape(block_tokens, heads_here, HD), my_places
    ).astype(jnp.bfloat16)
    half_raw = projected[:, query_cols:]
    rotated = rotate(half_raw[:, None, :], my_places)[:, 0, :]
    mine = jnp.where(is_key, rotated, half_raw).astype(jnp.bfloat16)

    first_blocks = [min(max(b - (window_blocks - 1), 0), count_gy - window_blocks) for b in range(count_gy)]
    chosen = jnp.asarray(
        [[f + w for w in range(window_blocks)] for f in first_blocks], dtype=jnp.int32
    )
    strided = mine.reshape(count_gy, sub, HD)
    kv_parcel = jnp.take(strided, chosen, axis=0).reshape(count_gy, window_blocks * sub, HD)
    q_parcel = queries.reshape(count_gy, sub * heads_here, HD)
    parcel = jnp.concatenate([q_parcel, kv_parcel], axis=1)
    arrived = lax.all_to_all(parcel, "gy", 0, 0, tiled=True)
    queries = arrived[:, : sub * heads_here].reshape(block_tokens, query_cols)
    mine_window = arrived[:, sub * heads_here :]
    other_window = lax.ppermute(mine_window, "gx", [(p, p ^ 1) for p in range(count_gx)])

    attention = segment_attention(
        is_key, queries, mine_window.reshape(window, HD), other_window.reshape(window, HD),
        q_segment, q_index, k_segment, k_index, HD,
    )

    cache_cols = lax.dynamic_index_in_dim(
        mine_window.reshape(count_gy, window_blocks, sub, HD), where_gy - window_first, 1, keepdims=False
    ).reshape(block_tokens, HD)
    pages_dev = PAGES_DEV
    page_len = block_tokens // pages_dev
    page_range = jnp.arange(pages_dev, dtype=jnp.int32)
    width_cols = cache_cols.shape[1]
    my_pages = cache_cols.reshape(pages_dev, page_len * width_cols)
    capacity = max(1, pages_dev // count_gy)
    slots_all = count_gy * capacity
    owners = (cache_slot // pages_dev).reshape(count_gy, pages_dev)
    earlier = page_range[None, :] < page_range[:, None]
    same_owner = owners[:, :, None] == owners[:, None, :]
    ranks = jnp.sum((same_owner & earlier[None]).astype(jnp.int32), axis=2)
    my_owner = lax.dynamic_index_in_dim(owners, where_gy, 0, keepdims=False)
    my_rank = lax.dynamic_index_in_dim(ranks, where_gy, 0, keepdims=False)
    target = my_owner * capacity + my_rank
    slot_range = jnp.arange(slots_all, dtype=jnp.int32)
    send_map = (slot_range[:, None] == target[None, :]).astype(jnp.bfloat16)
    outgoing = jnp.dot(send_map, my_pages, preferred_element_type=jnp.float32).astype(jnp.bfloat16)
    incoming = lax.all_to_all(outgoing, "gy", split_axis=0, concat_axis=0, tiled=True)
    wanted = where_gy * pages_dev + page_range
    matches = cache_slot[None, :] == wanted[:, None]
    page_ids = jnp.arange(cache_slot.shape[0], dtype=jnp.int32)
    source_page = jnp.sum(jnp.where(matches, page_ids[None, :], 0), axis=1)
    source_rank = jnp.sum(jnp.where(matches, ranks.reshape(-1)[None, :], 0), axis=1)
    source_slot = source_page // pages_dev * capacity + source_rank
    take_map = (source_slot[:, None] == slot_range[None, :]).astype(jnp.bfloat16)
    cache_block = jnp.dot(take_map, incoming, preferred_element_type=jnp.float32)
    cache_block = cache_block.astype(jnp.bfloat16).reshape(pages_dev, page_len, width_cols)
    return (attention, cache_block)


def solution(mesh):
    return jax.shard_map(
        local,
        mesh=mesh,
        in_specs=(P("gx", "gy"), P("gy"), P("gx", "gy"), P(None, "gy"), P(), P()),
        out_specs=(P("gy", "gx"), P("gy", None, "gx")),
        check_vma=False,
    )
```

```python
import functools
import math

import jax
import jax.numpy as jnp
from jax import lax
from jax.experimental import pallas as pl
from jax.experimental.pallas import tpu as pltpu
from jax.sharding import PartitionSpec as P


HD = 128
PAGES_DEV = 16
MOST = 4096


epsilon = 1e-06
rope_base = 5000000.0
masked_out = -1e30


def token_places(prompt_lengths, token_index):
    prompt_ends = jnp.cumsum(prompt_lengths)
    prompt_starts = prompt_ends - prompt_lengths
    segment = jnp.sum((token_index[:, None] >= prompt_ends[None, :]).astype(jnp.int32), axis=1)
    chosen = segment[:, None] == jnp.arange(prompt_lengths.shape[0], dtype=jnp.int32)[None, :]
    opening = jnp.sum(jnp.where(chosen, prompt_starts[None, :], 0), axis=1)
    return (segment, token_index - opening)


def rotate(vectors, places):
    half_size = vectors.shape[-1] // 2
    frequency = rope_base ** (-(jnp.arange(half_size, dtype=jnp.float32) * 2.0) / vectors.shape[-1])
    angles = places.astype(jnp.float32)[:, None] * frequency[None, :]
    cos_part = jnp.cos(angles)[:, None, :]
    sin_part = jnp.sin(angles)[:, None, :]
    leading = vectors[..., :half_size]
    trailing = vectors[..., half_size:]
    return jnp.concatenate(
        [leading * cos_part - trailing * sin_part, trailing * cos_part + leading * sin_part],
        axis=-1,
    )


def attention_heads(scale, heads, head_size, q_ref, k_ref, v_ref, allowed, o_ref):
    for h in range(heads):
        columns = slice(h * head_size, (h + 1) * head_size)
        scores = lax.dot_general(
            q_ref[:, columns], k_ref[...], (((1,), (1,)), ((), ())),
            preferred_element_type=jnp.float32,
        ) * scale
        scores = jnp.where(allowed, scores, masked_out)
        row_max = jnp.max(scores, axis=1, keepdims=True)
        weights = jnp.exp(scores - row_max)
        totals = jnp.sum(weights, axis=1, keepdims=True)
        mixed = jnp.dot(weights.astype(jnp.bfloat16), v_ref[...], preferred_element_type=jnp.float32)
        o_ref[:, columns] = (mixed / totals).astype(o_ref.dtype)


def attention_body(scale, heads, head_size, flag_ref, q_ref, a_ref, b_ref, qseg_ref, qidx_ref, kseg_ref, kidx_ref, o_ref):
    allowed = (kseg_ref[...] == qseg_ref[...]) & (kidx_ref[...] <= qidx_ref[...])

    @pl.when(flag_ref[0] == 1)
    def _():
        attention_heads(scale, heads, head_size, q_ref, a_ref, b_ref, allowed, o_ref)

    @pl.when(flag_ref[0] != 1)
    def _():
        attention_heads(scale, heads, head_size, q_ref, b_ref, a_ref, allowed, o_ref)


def segment_attention(a_is_key, queries, a_rows, b_rows, q_segment, q_index, k_segment, k_index, head_size, row_chunk=64):
    tokens, cols = queries.shape
    heads = cols // head_size
    window = a_rows.shape[0]
    flops = 4 * tokens * window * head_size * heads
    grid_spec = pltpu.PrefetchScalarGridSpec(
        num_scalar_prefetch=1,
        grid=(tokens // row_chunk,),
        in_specs=[
            pl.BlockSpec((row_chunk, cols), lambda r, f: (r, 0)),
            pl.BlockSpec((window, head_size), lambda r, f: (0, 0)),
            pl.BlockSpec((window, head_size), lambda r, f: (0, 0)),
            pl.BlockSpec((row_chunk, 1), lambda r, f: (r, 0)),
            pl.BlockSpec((row_chunk, 1), lambda r, f: (r, 0)),
            pl.BlockSpec((1, window), lambda r, f: (0, 0)),
            pl.BlockSpec((1, window), lambda r, f: (0, 0)),
        ],
        out_specs=pl.BlockSpec((row_chunk, cols), lambda r, f: (r, 0)),
    )
    return pl.pallas_call(
        functools.partial(attention_body, 1.0 / math.sqrt(head_size), heads, head_size),
        grid_spec=grid_spec,
        out_shape=jax.ShapeDtypeStruct((tokens, cols), jnp.bfloat16),
        cost_estimate=pl.CostEstimate(
            flops=flops, transcendentals=tokens * window * heads,
            bytes_accessed=2 * (2 * tokens * cols + 2 * window * head_size) + 8 * (tokens + window),
        ),
    )(a_is_key.astype(jnp.int32).reshape(1), queries, a_rows, b_rows, q_segment, q_index, k_segment, k_index)


def local(hidden_in, norm_gain, query_proj, kv_proj, prompt_lengths, cache_slot):
    count_gx = lax.axis_size("gx")
    count_gy = lax.axis_size("gy")
    where_gx = lax.axis_index("gx")
    where_gy = lax.axis_index("gy")
    local_rows, local_feats = hidden_in.shape
    features = local_feats * count_gy
    block_tokens = local_rows * count_gx // count_gy
    blocks_per_slab = local_rows // block_tokens
    sub = block_tokens // count_gy
    heads_here = query_proj.shape[0] // HD
    query_cols = heads_here * HD
    is_key = where_gx % 2 == 0

    kv_rows = lax.dynamic_slice_in_dim(kv_proj, where_gx * HD, HD, 0)
    gain_rows = jnp.concatenate(
        [norm_gain[None, :], jnp.zeros((7, local_feats), norm_gain.dtype)], axis=0
    )
    stacked = jnp.concatenate([query_proj, kv_rows, gain_rows], axis=0)
    gathered = lax.all_gather(stacked, "gy", axis=1, tiled=True)
    weight_rows = query_cols + HD
    weights_full = gathered[:weight_rows]
    gain_full = gathered[weight_rows]

    pieces = hidden_in.reshape(blocks_per_slab, count_gy, sub, local_feats)
    pieces = lax.all_to_all(pieces, "gy", 1, 1, tiled=True)
    spread = jnp.broadcast_to(pieces[None], (count_gx,) + pieces.shape)
    rows_here = lax.all_to_all(spread, "gx", 0, 0, tiled=True)
    rows_here = rows_here.transpose(0, 1, 3, 2, 4).reshape(block_tokens, features)
    needed_blocks = MOST // block_tokens + 1
    window_blocks = min(count_gy, -(-needed_blocks * sub // 16) * 16 // sub)
    window = window_blocks * block_tokens
    order = jnp.arange(block_tokens, dtype=jnp.int32)
    first_query = where_gy * block_tokens
    token_index = first_query + order
    segment_own, unused_places = token_places(prompt_lengths, token_index)
    window_first = jnp.clip(where_gy - (window_blocks - 1), 0, count_gy - window_blocks)
    source_range = jnp.arange(count_gy, dtype=jnp.int32)[:, None, None]
    block_range = jnp.arange(window_blocks, dtype=jnp.int32)[None, :, None]
    sub_range = jnp.arange(sub, dtype=jnp.int32)[None, None, :]
    key_index = (
        (window_first + block_range) * block_tokens + source_range * sub + sub_range
    ).reshape(window)
    key_segment, unused_places = token_places(prompt_lengths, key_index)
    q_segment = segment_own.reshape(block_tokens, 1)
    q_index = token_index.reshape(block_tokens, 1)
    k_segment = key_segment.reshape(1, window)
    k_index = key_index.reshape(1, window)
    pages_dev = PAGES_DEV
    page_len = block_tokens // pages_dev
    page_range = jnp.arange(pages_dev, dtype=jnp.int32)
    capacity = max(1, pages_dev // count_gy)
    slots_all = count_gy * capacity
    owners = (cache_slot // pages_dev).reshape(count_gy, pages_dev)
    earlier = page_range[None, :] < page_range[:, None]
    same_owner = owners[:, :, None] == owners[:, None, :]
    ranks = jnp.sum((same_owner & earlier[None]).astype(jnp.int32), axis=2)
    my_owner = lax.dynamic_index_in_dim(owners, where_gy, 0, keepdims=False)
    my_rank = lax.dynamic_index_in_dim(ranks, where_gy, 0, keepdims=False)
    target = my_owner * capacity + my_rank
    slot_range = jnp.arange(slots_all, dtype=jnp.int32)
    send_map = (slot_range[:, None] == target[None, :]).astype(jnp.bfloat16)
    wanted = where_gy * pages_dev + page_range
    matches = cache_slot[None, :] == wanted[:, None]
    page_ids = jnp.arange(cache_slot.shape[0], dtype=jnp.int32)
    source_page = jnp.sum(jnp.where(matches, page_ids[None, :], 0), axis=1)
    source_rank = jnp.sum(jnp.where(matches, ranks.reshape(-1)[None, :], 0), axis=1)
    source_slot = source_page // pages_dev * capacity + source_rank
    take_map = (source_slot[:, None] == slot_range[None, :]).astype(jnp.bfloat16)
    rows_here, q_segment, q_index, k_segment, k_index, send_map, take_map = lax.optimization_barrier(
        (rows_here, q_segment, q_index, k_segment, k_index, send_map, take_map)
    )
    widened = rows_here.astype(jnp.float32)
    squares = jnp.sum(widened * widened, axis=1)
    normed = (
        widened * lax.rsqrt(squares / features + epsilon)[:, None]
        * gain_full.astype(jnp.float32)[None, :]
    ).astype(jnp.bfloat16)
    contract = (((1,), (1,)), ((), ()))
    projected = lax.dot_general(normed, weights_full, contract, preferred_element_type=jnp.float32)

    my_tokens = (order // sub) * block_tokens + where_gy * sub + order % sub
    _, my_places = token_places(prompt_lengths, my_tokens)
    queries = rotate(
        projected[:, :query_cols].reshape(block_tokens, heads_here, HD), my_places
    ).astype(jnp.bfloat16)
    half_raw = projected[:, query_cols:]
    rotated = rotate(half_raw[:, None, :], my_places)[:, 0, :]
    mine = jnp.where(is_key, rotated, half_raw).astype(jnp.bfloat16)

    first_blocks = [min(max(b - (window_blocks - 1), 0), count_gy - window_blocks) for b in range(count_gy)]
    chosen = jnp.asarray(
        [[f + w for w in range(window_blocks)] for f in first_blocks], dtype=jnp.int32
    )
    strided = mine.reshape(count_gy, sub, HD)
    kv_parcel = jnp.take(strided, chosen, axis=0).reshape(count_gy, window_blocks * sub, HD)
    q_parcel = queries.reshape(count_gy, sub * heads_here, HD)
    parcel = jnp.concatenate([q_parcel, kv_parcel], axis=1)
    arrived = lax.all_to_all(parcel, "gy", 0, 0, tiled=True)
    queries = arrived[:, : sub * heads_here].reshape(block_tokens, query_cols)
    mine_window = arrived[:, sub * heads_here :]
    other_window = lax.ppermute(mine_window, "gx", [(p, p ^ 1) for p in range(count_gx)])

    attention = segment_attention(
        is_key, queries, mine_window.reshape(window, HD), other_window.reshape(window, HD),
        q_segment, q_index, k_segment, k_index, HD,
    )

    cache_cols = lax.dynamic_index_in_dim(
        mine_window.reshape(count_gy, window_blocks, sub, HD), where_gy - window_first, 1, keepdims=False
    ).reshape(block_tokens, HD)
    width_cols = cache_cols.shape[1]
    my_pages = cache_cols.reshape(pages_dev, page_len * width_cols)
    outgoing = jnp.dot(send_map, my_pages, preferred_element_type=jnp.float32).astype(jnp.bfloat16)
    incoming = lax.all_to_all(outgoing, "gy", split_axis=0, concat_axis=0, tiled=True)
    cache_block = jnp.dot(take_map, incoming, preferred_element_type=jnp.float32)
    cache_block = cache_block.astype(jnp.bfloat16).reshape(pages_dev, page_len, width_cols)
    return (attention, cache_block)


def solution(mesh):
    return jax.shard_map(
        local,
        mesh=mesh,
        in_specs=(P("gx", "gy"), P("gy"), P("gx", "gy"), P(None, "gy"), P(), P()),
        out_specs=(P("gy", "gx"), P("gy", None, "gx")),
        check_vma=False,
    )
```
